256 devices in a mesh: seq: 64 (over x, z, core), tensor: 4 (over y).
Axes of the slice: x: 4, y: 4, z: 8, core: 2. Of those that a mesh axis runs over, the one named last changes fastest.
Arguments:
- hidden: bfloat16 [512, 1280], P('seq', 'tensor'), may hold values from -20 to 20
- inward_weight: bfloat16 [1280, 3, 1280], P(None, None, 'tensor'), may hold values from -0.15625 to 0.15625
- output_weight: bfloat16 [1280, 1280], P('tensor'), may hold values from -0.559017 to 0.559017
- score_gain: float32 [1280], P('tensor'), may hold values from 0.5 to 9
- eigen_rate: float32 [1280], replicated, may hold values from 0.1 to 0.6
- lengths: int32 [512], replicated, may hold values from 1 to 16384, as said below
- page_request: int32 [1536], P('seq'), may hold values from 0 to 511, as said below
- page_number: int32 [1536], P('seq'), may hold values from 0 to 128, as said below
- page_cache: bfloat16 [1536, 128, 2, 1280], P('seq', None, None, 'tensor'), may hold values from -6 to 6
Outputs:
- new_hidden: bfloat16 [512, 1280], P('seq', 'tensor')
The draws below stay inside these ranges and needn't reach their ends.
Inputs may be any that keep to these rules, and one draw needn't show every extreme that they name: `lengths`: exactly 4 requests have more than 256 cached positions; they have more than 16256, one has exactly 16384. Every other request has at most 256, one exactly 256. `page_request`: each page of each request stands in exactly one slot: pages 0 to 1 of every short request, pages 0 to 127 of every long request. The remaining 2 * 4 slots name a long request with page number 128 and hold nothing live. `page_number`: see page_request.
All inputs are finite; a program needn't handle non-finite values.
Results may differ from the reference program's by a relative error of at most 0.012.
The reference program's roundings to bfloat16 on the way count: a program that leaves them out, or rounds other values in their place, can miss the bound.
Values may be sent and summed in bfloat16 or wider, within the bound.
No kernel may reach another device: no remote copies, remote signals or barrier semaphores. Data moves between devices by JAX's collectives and lax.ppermute only.
A program may use at most 192 MiB of HBM per device.

```python
import math
import jax
import jax.numpy as jnp
from jax import lax

D = 1280
HEADS = 20
HEAD_DIM = 64
PAGE = 128
SHORT_PAGES = 2
LONG = 4
REQUESTS = 512
SHORT_LEN = 256
LONG_PAGES = 128
LONG_LEN = 16384
POOL_DEV = 24
POOL = 1536
N_SEQ = 64


def page_layout(key):
    key = jax.random.fold_in(key, 17)
    keys = jax.random.split(key, 5)
    order = jax.random.permutation(keys[0], REQUESTS).astype(jnp.int32)
    rank = jnp.zeros((REQUESTS,), jnp.int32).at[order].set(jnp.arange(REQUESTS, dtype=jnp.int32))
    is_long = rank < LONG
    level = jax.random.randint(keys[1], (REQUESTS,), 0, 4).astype(jnp.int32)
    ceiling = jnp.right_shift(jnp.full((REQUESTS,), SHORT_LEN, jnp.int32), 3 - level)
    short_len = jax.random.randint(keys[2], (REQUESTS,), 1, ceiling + 1).astype(jnp.int32)
    short_len = jnp.where(rank == LONG, SHORT_LEN, short_len)
    long_len = jnp.where(rank == 0, LONG_LEN, LONG_LEN - jax.random.randint(keys[3], (REQUESTS,), 0, PAGE))
    lengths = jnp.where(is_long, long_len, short_len).astype(jnp.int32)
    short_owner = jnp.repeat(jnp.arange(REQUESTS, dtype=jnp.int32), SHORT_PAGES)
    short_number = jnp.tile(jnp.arange(SHORT_PAGES, dtype=jnp.int32), REQUESTS)
    short_number = jnp.where(is_long[short_owner], LONG_PAGES, short_number)
    long_owner = jnp.repeat(order[:LONG], LONG_PAGES)
    long_number = jnp.tile(jnp.arange(LONG_PAGES, dtype=jnp.int32), LONG)
    owners = jnp.concatenate([short_owner, long_owner]).astype(jnp.int32)
    numbers = jnp.concatenate([short_number, long_number]).astype(jnp.int32)
    shuffle = jax.random.permutation(keys[4], POOL)
    return (lengths, owners[shuffle], numbers[shuffle])


def draw_lengths(key, part):
    return page_layout(key)[0]


def draw_page_request(key, part):
    return page_layout(key)[1]


def draw_page_number(key, part):
    return page_layout(key)[2]


def draw_score_gain(key, part):
    return jnp.exp(jax.random.uniform(key, (D,), jnp.float32, jnp.log(0.5), jnp.log(2.0))).astype(jnp.float32)


def draw_output_weight(key, part):
    key = jax.random.fold_in(key, 29)
    base = jnp.clip(jax.random.normal(key, (D, D), jnp.float32), -6.0, 6.0)
    column = jnp.arange(D, dtype=jnp.float32) / (D - 1.0) - 0.5
    rise = jnp.exp(jnp.log(10.0) * column)
    return (base * rise[None, :] / jnp.sqrt(jnp.float32(D))).astype(jnp.bfloat16)


def draw_hidden(key, part):
    key = jax.random.fold_in(key, 41)
    column = jnp.arange(D, dtype=jnp.float32) / (D - 1.0) - 0.5
    base = jnp.clip(jax.random.normal(key, (REQUESTS, D), jnp.float32), -6.0, 6.0)
    rise = jnp.exp(jnp.log(10.0) * column)
    return (base * rise[None, :]).astype(jnp.bfloat16)


def levels(own_key, extent, pieces, least, high):
    def one(axis_at, parts):
        steps = jax.random.uniform(jax.random.fold_in(jax.random.fold_in(own_key, 6), axis_at), (parts,), jnp.float32, least / len(pieces), high / len(pieces))
        return jnp.repeat(jnp.exp(steps), extent[axis_at] // parts).reshape((-1,) + (1,) * (len(extent) - axis_at - 1))

    loudness = one(*pieces[0])
    for cut in pieces[1:]:
        loudness = loudness * one(*cut)
    return loudness


def scatter_about(key, shape, spread, most, cuts=(), held_as=jnp.bfloat16):
    level = levels(key, shape, cuts, -0.22, 0.18) if cuts else 1.0
    drawn = jax.random.normal(key, shape, jnp.float32) * spread * level
    return jnp.minimum(jnp.maximum(drawn, -most), most).astype(held_as)


def setup_inputs(seed: int = 0) -> dict:
    seeds = jax.random.split(jax.random.key(seed), 10)
    hidden = draw_hidden(jax.random.fold_in(seeds[9], 71), 0)
    inward_weight = scatter_about(seeds[1], (D, 3, D), D ** -0.5, 0.15625, ((2, 4),))
    output_weight = draw_output_weight(jax.random.fold_in(seeds[9], 71), 0)
    score_gain = draw_score_gain(jax.random.fold_in(seeds[9], 71), 0)
    eigen_rate = jnp.clip(jnp.exp(jax.random.uniform(seeds[4], (D,), jnp.float32, math.log(0.1), math.log(0.6))), 0.1, 0.6)
    lengths = draw_lengths(jax.random.fold_in(seeds[9], 71), 0)
    page_request = draw_page_request(jax.random.fold_in(seeds[9], 71), 0)
    page_number = draw_page_number(jax.random.fold_in(seeds[9], 71), 0)
    page_cache = scatter_about(seeds[8], (POOL, PAGE, 2, D), 1.0, 6.0, ((0, 64), (3, 4)))
    return dict(hidden=hidden, inward_weight=inward_weight, output_weight=output_weight, score_gain=score_gain, eigen_rate=eigen_rate, lengths=lengths, page_request=page_request, page_number=page_number, page_cache=page_cache)


epsilon = 1e-06
far_below = -1e+30

def head_norm(values, gain):
    shaped = values.reshape(values.shape[:-1] + (-1, HEAD_DIM))
    normed = shaped / jnp.sqrt(lax.optimization_barrier(jnp.mean(shaped * shaped, axis=-1, keepdims=True)) + epsilon)
    return normed * gain.reshape(-1, HEAD_DIM)

def reference(hidden, inward_weight, output_weight, score_gain, eigen_rate, lengths, page_request, page_number, page_cache):
    projected = jnp.dot(hidden, inward_weight.reshape(D, 3 * D), preferred_element_type=jnp.float32).reshape(REQUESTS, 3, D)
    query = head_norm(projected[:, 0], score_gain).astype(jnp.bfloat16)
    key_new = head_norm(projected[:, 1], score_gain).astype(jnp.bfloat16)
    value_own = projected[:, 2].reshape(REQUESTS, HEADS, HEAD_DIM).astype(jnp.bfloat16)
    own_score = lax.optimization_barrier(jnp.sum(query.astype(jnp.float32) * key_new.astype(jnp.float32), axis=-1)) / math.sqrt(HEAD_DIM)

    def page_parts(block):
        cache_block, owner_block, number_block = block
        count = cache_block.shape[0]
        keys_scaled = head_norm(cache_block[:, :, 0, :].astype(jnp.float32), score_gain).astype(jnp.bfloat16)
        values_paged = cache_block[:, :, 1, :].reshape(count, PAGE, HEADS, HEAD_DIM)
        owner_query = query[owner_block]
        scores = jnp.einsum('sphd,shd->shp', keys_scaled.astype(jnp.float32), owner_query.astype(jnp.float32)) / math.sqrt(HEAD_DIM)
        positions = number_block[:, None] * PAGE + jnp.arange(PAGE, dtype=jnp.int32)[None, :]
        live_mask = positions < lengths[owner_block][:, None]
        page_max = lax.optimization_barrier(jnp.max(jnp.where(live_mask[:, None, :], scores, far_below), axis=-1))
        weights = jnp.where(live_mask[:, None, :], jnp.exp(scores - page_max[..., None]), 0.0).astype(jnp.bfloat16)
        page_total = lax.optimization_barrier(jnp.sum(weights.astype(jnp.float32), axis=-1))
        page_acc = jnp.einsum('shp,sphd->shd', weights.astype(jnp.float32), values_paged.astype(jnp.float32))
        return (page_max, page_total, page_acc)
    blocks = (page_cache.reshape(N_SEQ, POOL_DEV, PAGE, 2, D), page_request.reshape(N_SEQ, POOL_DEV), page_number.reshape(N_SEQ, POOL_DEV))
    page_max, page_total, page_acc = lax.map(page_parts, blocks)
    page_max = page_max.reshape(POOL, HEADS)
    page_total = page_total.reshape(POOL, HEADS)
    page_acc = page_acc.reshape(POOL, HEADS, HEAD_DIM)
    row_max = own_score.at[page_request].max(page_max)
    factor = jnp.exp(page_max - row_max[page_request])
    own_factor = jnp.exp(own_score - row_max)
    total = own_factor + jax.ops.segment_sum(page_total * factor, page_request, REQUESTS)
    summed = value_own.astype(jnp.float32) * own_factor[..., None] + jax.ops.segment_sum(page_acc * factor[..., None], page_request, REQUESTS)
    attended = (summed / total[..., None]).astype(jnp.bfloat16).reshape(REQUESTS, D)
    attn_out = jnp.dot(attended, output_weight, preferred_element_type=jnp.float32)
    state = hidden.astype(jnp.float32)
    unit = attn_out / jnp.sqrt(lax.optimization_barrier(jnp.mean(attn_out * attn_out, axis=-1, keepdims=True)) + epsilon)
    mixed = state + eigen_rate * (unit - state)
    return (mixed / jnp.sqrt(lax.optimization_barrier(jnp.mean(mixed * mixed, axis=-1, keepdims=True)) + epsilon)).astype(jnp.bfloat16)
```

```python
import math

import jax
import jax.numpy as jnp
from jax import lax
from jax.sharding import PartitionSpec as P

HEAD_DIM = 64


epsilon = 1e-06
far_below = -1e30


def head_norm(values, gain):
    shaped = values.reshape(values.shape[:-1] + (-1, HEAD_DIM))
    normed = shaped / jnp.sqrt(jnp.mean(shaped * shaped, axis=-1, keepdims=True) + epsilon)
    return normed * gain.reshape(-1, HEAD_DIM)


def scale_heads(summed, factor):
    shaped = summed.reshape(summed.shape[:-1] + (factor.shape[-1], -1))
    return (shaped * factor[..., None]).reshape(summed.shape)


def local(
    hidden,
    inward_weight,
    output_weight,
    score_gain,
    eigen_rate,
    lengths,
    page_request,
    page_number,
    page_cache,
):
    rows, width_local = hidden.shape
    heads_local = width_local // HEAD_DIM
    gathered = lax.all_gather(hidden, "tensor", axis=1, tiled=True)
    projected = jnp.dot(
        gathered,
        inward_weight.reshape(inward_weight.shape[0], -1),
        preferred_element_type=jnp.float32,
    )
    query = head_norm(projected[:, :width_local], score_gain).astype(jnp.bfloat16)
    key_new = head_norm(projected[:, width_local : 2 * width_local], score_gain).astype(
        jnp.bfloat16
    )
    value_own = projected[:, 2 * width_local :].astype(jnp.bfloat16)
    own_score = jnp.sum(
        (query.astype(jnp.float32) * key_new.astype(jnp.float32)).reshape(
            rows, heads_local, HEAD_DIM
        ),
        axis=-1,
    ) / math.sqrt(HEAD_DIM)

    all_queries = lax.all_gather(query, "seq", axis=0, tiled=True)
    pages, page_len = (page_cache.shape[0], page_cache.shape[1])
    owner_query = all_queries[page_request].reshape(pages, heads_local, HEAD_DIM)
    keys_scaled = head_norm(page_cache[:, :, 0, :].astype(jnp.float32), score_gain).astype(
        jnp.bfloat16
    )
    values_paged = page_cache[:, :, 1, :].reshape(pages, page_len, heads_local, HEAD_DIM)
    scores = jnp.einsum(
        "sphd,shd->shp", keys_scaled, owner_query, preferred_element_type=jnp.float32
    ) / math.sqrt(HEAD_DIM)
    positions = page_number[:, None] * page_len + jnp.arange(page_len, dtype=jnp.int32)[None, :]
    live_mask = positions < lengths[page_request][:, None]
    page_max = jnp.max(jnp.where(live_mask[:, None, :], scores, far_below), axis=-1)
    weights = jnp.where(live_mask[:, None, :], jnp.exp(scores - page_max[..., None]), 0.0).astype(
        jnp.bfloat16
    )
    page_total = jnp.sum(weights.astype(jnp.float32), axis=-1)
    page_acc = jnp.einsum(
        "shp,sphd->shd", weights, values_paged, preferred_element_type=jnp.float32
    ).reshape(pages, width_local)

    packed = jnp.concatenate(
        [page_acc, page_total, page_max, page_request.astype(jnp.float32)[:, None]], axis=1
    )
    all_parts = lax.all_gather(packed, "seq", axis=0, tiled=True)
    acc_all = all_parts[:, :width_local]
    total_all = all_parts[:, width_local : width_local + heads_local]
    max_all = all_parts[:, width_local + heads_local : width_local + 2 * heads_local]
    owner_all = all_parts[:, width_local + 2 * heads_local]

    first_row = lax.axis_index("seq") * rows
    row_ids = (first_row + jnp.arange(rows, dtype=jnp.int32)).astype(jnp.float32)
    mine = owner_all[None, :] == row_ids[:, None]
    masked_max = jnp.max(jnp.where(mine[:, :, None], max_all[None], far_below), axis=1)
    final_max = jnp.maximum(masked_max, own_score)
    factor = jnp.where(
        mine[:, :, None], jnp.exp(max_all[None] - final_max[:, None, :]), 0.0
    )
    own_factor = jnp.exp(own_score - final_max)
    total = jnp.sum(factor * total_all[None], axis=1) + own_factor
    stored = jnp.einsum(
        "rsh,shd->rhd",
        factor,
        acc_all.reshape(-1, heads_local, HEAD_DIM),
        precision=lax.Precision.HIGHEST,
    ).reshape(rows, width_local)
    summed = stored + scale_heads(value_own.astype(jnp.float32), own_factor)
    attended = (
        (summed.reshape(rows, heads_local, HEAD_DIM) / total[..., None])
        .reshape(rows, width_local)
        .astype(jnp.bfloat16)
    )
    partial_out = jnp.dot(attended, output_weight, preferred_element_type=jnp.float32)
    attn_out = lax.psum(partial_out, "tensor")
    width = attn_out.shape[1]
    state = gathered.astype(jnp.float32)
    unit = attn_out / jnp.sqrt(jnp.sum(attn_out * attn_out, axis=-1, keepdims=True) / width + epsilon)
    mixed = state + eigen_rate * (unit - state)
    result = mixed / jnp.sqrt(jnp.sum(mixed * mixed, axis=-1, keepdims=True) / width + epsilon)
    first_col = lax.axis_index("tensor") * width_local
    return lax.dynamic_slice_in_dim(result, first_col, width_local, 1).astype(jnp.bfloat16)


def solution(mesh):
    placed = (
        P("seq", "tensor"),
        P(None, None, "tensor"),
        P("tensor", None),
        P("tensor"),
        P(),
        P(),
        P("seq"),
        P("seq"),
        P("seq", None, None, "tensor"),
    )
    return jax.shard_map(
        local, mesh=mesh, in_specs=placed, out_specs=P("seq", "tensor"), check_vma=False
    )
```

```python
import math

import jax
import jax.numpy as jnp
from jax import lax
from jax.sharding import PartitionSpec as P

HEAD_DIM = 64


epsilon = 1e-06
far_below = -1e30


def head_norm(values, gain):
    shaped = values.reshape(values.shape[:-1] + (-1, HEAD_DIM))
    normed = shaped / jnp.sqrt(jnp.mean(shaped * shaped, axis=-1, keepdims=True) + epsilon)
    return normed * gain.reshape(-1, HEAD_DIM)


def scale_heads(summed, factor):
    shaped = summed.reshape(summed.shape[:-1] + (factor.shape[-1], -1))
    return (shaped * factor[..., None]).reshape(summed.shape)


def xor_partner(axis, size, bit):
    return [(i, i ^ bit) for i in range(size)]


def gather_doubling(value, axis):
    size = lax.axis_size(axis)
    index = lax.axis_index(axis)
    held = value[None]
    bit = 1
    while bit < size:
        other = lax.ppermute(held, axis, perm=xor_partner(axis, size, bit))
        high = (index & bit) != 0
        held = jnp.where(high, jnp.stack([other, held]), jnp.stack([held, other]))
        held = held.reshape((-1,) + value.shape)
        bit *= 2
    return held


def sum_doubling(value, axis):
    size = lax.axis_size(axis)
    bit = 1
    while bit < size:
        value = value + lax.ppermute(value, axis, perm=xor_partner(axis, size, bit))
        bit *= 2
    return value


def merge_packed(first, second, width, heads):
    first_acc, first_total, first_max = (
        first[..., :width], first[..., width : width + heads], first[..., width + heads :]
    )
    second_acc, second_total, second_max = (
        second[..., :width], second[..., width : width + heads], second[..., width + heads :]
    )
    top = jnp.maximum(first_max, second_max)
    first_factor = jnp.exp(first_max - top)
    second_factor = jnp.exp(second_max - top)
    return jnp.concatenate(
        [
            scale_heads(first_acc, first_factor) + scale_heads(second_acc, second_factor),
            first_total * first_factor + second_total * second_factor,
            top,
        ],
        axis=-1,
    )


def scatter_halving(packed, axis, width, heads):
    size = lax.axis_size(axis)
    index = lax.axis_index(axis)
    bit = 1
    step = 0
    while bit < size:
        paired = packed.reshape((packed.shape[0] // 2, 2) + packed.shape[1:])
        mine = (index >> step) & 1
        keep = lax.dynamic_index_in_dim(paired, mine, 1, False)
        send = lax.dynamic_index_in_dim(paired, 1 - mine, 1, False)
        other = lax.ppermute(send, axis, perm=xor_partner(axis, size, bit))
        packed = merge_packed(keep, other, width, heads)
        bit *= 2
        step += 1
    return packed[0]


def local(
    hidden,
    inward_weight,
    output_weight,
    score_gain,
    eigen_rate,
    lengths,
    page_request,
    page_number,
    page_cache,
):
    rows, width_local = hidden.shape
    heads_local = width_local // HEAD_DIM
    gathered = jnp.moveaxis(gather_doubling(hidden, "tensor"), 0, 1).reshape(rows, -1)
    projected = jnp.dot(
        gathered,
        inward_weight.reshape(inward_weight.shape[0], -1),
        preferred_element_type=jnp.float32,
    )
    query = head_norm(projected[:, :width_local], score_gain).astype(jnp.bfloat16)
    key_new = head_norm(projected[:, width_local : 2 * width_local], score_gain).astype(
        jnp.bfloat16
    )
    value_own = projected[:, 2 * width_local :].astype(jnp.bfloat16)
    own_score = jnp.sum(
        (query.astype(jnp.float32) * key_new.astype(jnp.float32)).reshape(
            rows, heads_local, HEAD_DIM
        ),
        axis=-1,
    ) / math.sqrt(HEAD_DIM)

    all_queries = gather_doubling(query, "seq").reshape(-1, width_local)
    pages, page_len = (page_cache.shape[0], page_cache.shape[1])
    owner_query = all_queries[page_request].reshape(pages, heads_local, HEAD_DIM)
    keys_scaled = head_norm(page_cache[:, :, 0, :].astype(jnp.float32), score_gain).astype(
        jnp.bfloat16
    )
    values_paged = page_cache[:, :, 1, :].reshape(pages, page_len, heads_local, HEAD_DIM)
    scores = jnp.einsum(
        "sphd,shd->shp", keys_scaled, owner_query, preferred_element_type=jnp.float32
    ) / math.sqrt(HEAD_DIM)
    positions = page_number[:, None] * page_len + jnp.arange(page_len, dtype=jnp.int32)[None, :]
    live_mask = positions < lengths[page_request][:, None]
    page_max = jnp.max(jnp.where(live_mask[:, None, :], scores, far_below), axis=-1)
    weights = jnp.where(live_mask[:, None, :], jnp.exp(scores - page_max[..., None]), 0.0).astype(
        jnp.bfloat16
    )
    page_total = jnp.sum(weights.astype(jnp.float32), axis=-1)
    page_acc = jnp.einsum(
        "shp,sphd->shd", weights, values_paged, preferred_element_type=jnp.float32
    ).reshape(pages, width_local)

    requests = lengths.shape[0]
    onehot = page_request[:, None] == jnp.arange(requests, dtype=jnp.int32)[None, :]
    request_max = jnp.max(jnp.where(onehot[:, :, None], page_max[:, None, :], far_below), axis=0)
    factor = jnp.exp(page_max - request_max[page_request])
    selector = onehot.astype(jnp.float32)
    request_total = jnp.dot(selector.T, page_total * factor, precision=lax.Precision.HIGHEST)
    request_acc = jnp.dot(
        selector.T, scale_heads(page_acc, factor), precision=lax.Precision.HIGHEST
    )
    packed = jnp.concatenate([request_acc, request_total, request_max], axis=1)
    packed = packed.reshape(lax.axis_size("seq"), rows, packed.shape[-1])
    home = scatter_halving(packed, "seq", width_local, heads_local)
    home_acc = home[:, :width_local]
    home_total = home[:, width_local : width_local + heads_local]
    home_max = home[:, width_local + heads_local :]
    final_max = jnp.maximum(home_max, own_score)
    stored_factor = jnp.exp(home_max - final_max)
    total_stored = home_total * stored_factor
    stored = scale_heads(home_acc, stored_factor)
    own_factor = jnp.exp(own_score - final_max)
    total = total_stored + own_factor
    summed = stored + scale_heads(value_own.astype(jnp.float32), own_factor)
    attended = (
        (summed.reshape(rows, heads_local, HEAD_DIM) / total[..., None])
        .reshape(rows, width_local)
        .astype(jnp.bfloat16)
    )
    partial_out = jnp.dot(attended, output_weight, preferred_element_type=jnp.float32)
    attn_out = sum_doubling(partial_out, "tensor")
    width = attn_out.shape[1]
    state = gathered.astype(jnp.float32)
    unit = attn_out / jnp.sqrt(jnp.sum(attn_out * attn_out, axis=-1, keepdims=True) / width + epsilon)
    mixed = state + eigen_rate * (unit - state)
    result = mixed / jnp.sqrt(jnp.sum(mixed * mixed, axis=-1, keepdims=True) / width + epsilon)
    first_col = lax.axis_index("tensor") * width_local
    return lax.dynamic_slice_in_dim(result, first_col, width_local, 1).astype(jnp.bfloat16)


def solution(mesh):
    placed = (
        P("seq", "tensor"),
        P(None, None, "tensor"),
        P("tensor", None),
        P("tensor"),
        P(),
        P(),
        P("seq"),
        P("seq"),
        P("seq", None, None, "tensor"),
    )
    return jax.shard_map(
        local, mesh=mesh, in_specs=placed, out_specs=P("seq", "tensor"), check_vma=False
    )
```

```python
import math

import jax
import jax.numpy as jnp
from jax import lax
from jax.sharding import PartitionSpec as P

HEAD_DIM = 64


epsilon = 1e-06
far_below = -1e30


def head_norm(values, gain):
    shaped = values.reshape(values.shape[:-1] + (-1, HEAD_DIM))
    normed = shaped / jnp.sqrt(jnp.mean(shaped * shaped, axis=-1, keepdims=True) + epsilon)
    return normed * gain.reshape(-1, HEAD_DIM)


def scale_heads(summed, factor):
    shaped = summed.reshape(summed.shape[:-1] + (factor.shape[-1], -1))
    return (shaped * factor[..., None]).reshape(summed.shape)


def xor_partner(axis, size, bit):
    return [(i, i ^ bit) for i in range(size)]


def digit_groups(size):
    groups = []
    while size > 1:
        width = 2 if size % 4 == 0 else 1
        groups.append(width)
        size >>= width
    return groups


def exchange(held, axis, low, width):
    size = lax.axis_size(axis)
    mine = (lax.axis_index(axis) >> low) & ((1 << width) - 1)
    got = [held] + [
        lax.ppermute(held, axis, perm=xor_partner(axis, size, digit << low))
        for digit in range(1, 1 << width)
    ]
    order = jnp.arange(1 << width, dtype=jnp.int32) ^ mine
    return jnp.take(jnp.stack(got), order, axis=0)


def gather_radix(value, axis):
    held = value[None]
    low = 0
    for width in digit_groups(lax.axis_size(axis)):
        held = exchange(held, axis, low, width).reshape((-1,) + value.shape)
        low += width
    return held


def sum_radix(value, axis):
    low = 0
    for width in digit_groups(lax.axis_size(axis)):
        stacked = exchange(value, axis, low, width)
        value = stacked[0]
        for digit in range(1, stacked.shape[0]):
            value = value + stacked[digit]
        low += width
    return value


def scatter_radix(packed, axis, width_acc, heads):
    size = lax.axis_size(axis)
    index = lax.axis_index(axis)
    low = 0
    for width in digit_groups(size):
        count = 1 << width
        mine = (index >> low) & (count - 1)
        grouped = packed.reshape((packed.shape[0] // count, count) + packed.shape[1:])
        pieces = [lax.dynamic_index_in_dim(grouped, mine, 1, False)]
        for digit in range(1, count):
            send = lax.dynamic_index_in_dim(grouped, mine ^ digit, 1, False)
            pieces.append(lax.ppermute(send, axis, perm=xor_partner(axis, size, digit << low)))
        stacked = jnp.stack(pieces)
        acc = stacked[..., :width_acc]
        total = stacked[..., width_acc : width_acc + heads]
        top_each = stacked[..., width_acc + heads :]
        top = jnp.max(top_each, axis=0)
        factor = jnp.exp(top_each - top[None])
        acc = jnp.sum(scale_heads(acc, factor), axis=0)
        total = jnp.sum(total * factor, axis=0)
        packed = jnp.concatenate([acc, total, top], axis=-1)
        low += width
    return packed[0]


def local(
    hidden,
    inward_weight,
    output_weight,
    score_gain,
    eigen_rate,
    lengths,
    page_request,
    page_number,
    page_cache,
):
    rows, width_local = hidden.shape
    heads_local = width_local // HEAD_DIM
    gathered = jnp.moveaxis(gather_radix(hidden, "tensor"), 0, 1).reshape(rows, -1)
    projected = jnp.dot(
        gathered,
        inward_weight.reshape(inward_weight.shape[0], -1),
        preferred_element_type=jnp.float32,
    )
    query = head_norm(projected[:, :width_local], score_gain).astype(jnp.bfloat16)
    key_new = head_norm(projected[:, width_local : 2 * width_local], score_gain).astype(
        jnp.bfloat16
    )
    value_own = projected[:, 2 * width_local :].astype(jnp.bfloat16)
    own_score = jnp.sum(
        (query.astype(jnp.float32) * key_new.astype(jnp.float32)).reshape(
            rows, heads_local, HEAD_DIM
        ),
        axis=-1,
    ) / math.sqrt(HEAD_DIM)

    all_queries = gather_radix(query, "seq").reshape(-1, width_local)
    pages, page_len = (page_cache.shape[0], page_cache.shape[1])
    owner_query = all_queries[page_request].reshape(pages, heads_local, HEAD_DIM)
    keys_scaled = head_norm(page_cache[:, :, 0, :].astype(jnp.float32), score_gain).astype(
        jnp.bfloat16
    )
    values_paged = page_cache[:, :, 1, :].reshape(pages, page_len, heads_local, HEAD_DIM)
    scores = jnp.einsum(
        "sphd,shd->shp", keys_scaled, owner_query, preferred_element_type=jnp.float32
    ) / math.sqrt(HEAD_DIM)
    positions = page_number[:, None] * page_len + jnp.arange(page_len, dtype=jnp.int32)[None, :]
    live_mask = positions < lengths[page_request][:, None]
    page_max = jnp.max(jnp.where(live_mask[:, None, :], scores, far_below), axis=-1)
    weights = jnp.where(live_mask[:, None, :], jnp.exp(scores - page_max[..., None]), 0.0).astype(
        jnp.bfloat16
    )
    page_total = jnp.sum(weights.astype(jnp.float32), axis=-1)
    page_acc = jnp.einsum(
        "shp,sphd->shd", weights, values_paged, preferred_element_type=jnp.float32
    ).reshape(pages, width_local)

    requests = lengths.shape[0]
    onehot = page_request[:, None] == jnp.arange(requests, dtype=jnp.int32)[None, :]
    request_max = jnp.max(jnp.where(onehot[:, :, None], page_max[:, None, :], far_below), axis=0)
    factor = jnp.exp(page_max - request_max[page_request])
    selector = onehot.astype(jnp.float32)
    request_total = jnp.dot(selector.T, page_total * factor, precision=lax.Precision.HIGHEST)
    request_acc = jnp.dot(
        selector.T, scale_heads(page_acc, factor), precision=lax.Precision.HIGHEST
    )
    packed = jnp.concatenate([request_acc, request_total, request_max], axis=1)
    packed = packed.reshape(lax.axis_size("seq"), rows, packed.shape[-1])
    home = scatter_radix(packed, "seq", width_local, heads_local)
    home_acc = home[:, :width_local]
    home_total = home[:, width_local : width_local + heads_local]
    home_max = home[:, width_local + heads_local :]
    final_max = jnp.maximum(home_max, own_score)
    stored_factor = jnp.exp(home_max - final_max)
    total_stored = home_total * stored_factor
    stored = scale_heads(home_acc, stored_factor)
    own_factor = jnp.exp(own_score - final_max)
    total = total_stored + own_factor
    summed = stored + scale_heads(value_own.astype(jnp.float32), own_factor)
    attended = (
        (summed.reshape(rows, heads_local, HEAD_DIM) / total[..., None])
        .reshape(rows, width_local)
        .astype(jnp.bfloat16)
    )
    partial_out = jnp.dot(attended, output_weight, preferred_element_type=jnp.float32)
    attn_out = sum_radix(partial_out, "tensor")
    width = attn_out.shape[1]
    state = gathered.astype(jnp.float32)
    unit = attn_out / jnp.sqrt(jnp.sum(attn_out * attn_out, axis=-1, keepdims=True) / width + epsilon)
    mixed = state + eigen_rate * (unit - state)
    result = mixed / jnp.sqrt(jnp.sum(mixed * mixed, axis=-1, keepdims=True) / width + epsilon)
    first_col = lax.axis_index("tensor") * width_local
    return lax.dynamic_slice_in_dim(result, first_col, width_local, 1).astype(jnp.bfloat16)


def solution(mesh):
    placed = (
        P("seq", "tensor"),
        P(None, None, "tensor"),
        P("tensor", None),
        P("tensor"),
        P(),
        P(),
        P("seq"),
        P("seq"),
        P("seq", None, None, "tensor"),
    )
    return jax.shard_map(
        local, mesh=mesh, in_specs=placed, out_specs=P("seq", "tensor"), check_vma=False
    )
```

```python
import math

import jax
import jax.numpy as jnp
from jax import lax
from jax.sharding import PartitionSpec as P

HEAD_DIM = 64


epsilon = 1e-06
far_below = -1e30


def head_norm(values, gain):
    shaped = values.reshape(values.shape[:-1] + (-1, HEAD_DIM))
    normed = shaped / jnp.sqrt(jnp.mean(shaped * shaped, axis=-1, keepdims=True) + epsilon)
    return normed * gain.reshape(-1, HEAD_DIM)


def scale_heads(summed, factor):
    shaped = summed.reshape(summed.shape[:-1] + (factor.shape[-1], -1))
    return (shaped * factor[..., None]).reshape(summed.shape)


def xor_partner(axis, size, bit):
    return [(i, i ^ bit) for i in range(size)]


def digit_groups(size):
    groups = []
    while size > 1:
        width = 2 if size % 4 == 0 else 1
        groups.append(width)
        size >>= width
    return groups


def exchange(held, axis, low, width):
    size = lax.axis_size(axis)
    mine = (lax.axis_index(axis) >> low) & ((1 << width) - 1)
    got = [held] + [
        lax.ppermute(held, axis, perm=xor_partner(axis, size, digit << low))
        for digit in range(1, 1 << width)
    ]
    order = jnp.arange(1 << width, dtype=jnp.int32) ^ mine
    return jnp.take(jnp.stack(got), order, axis=0)


def gather_radix(value, axis):
    held = value[None]
    low = 0
    for width in digit_groups(lax.axis_size(axis)):
        held = exchange(held, axis, low, width).reshape((-1,) + value.shape)
        low += width
    return held


def gather_xor(value, axis):
    size = lax.axis_size(axis)
    held = value[None]
    low = 0
    for width in digit_groups(size):
        got = [held] + [
            lax.ppermute(held, axis, perm=xor_partner(axis, size, digit << low))
            for digit in range(1, 1 << width)
        ]
        held = jnp.stack(got).reshape((-1,) + value.shape)
        low += width
    return held


def scatter_xor(packed, axis, width_acc, heads):
    size = lax.axis_size(axis)
    low = 0
    for width in digit_groups(size):
        count = 1 << width
        grouped = packed.reshape((packed.shape[0] // count, count) + packed.shape[1:])
        pieces = [grouped[:, 0]]
        for digit in range(1, count):
            pieces.append(
                lax.ppermute(grouped[:, digit], axis, perm=xor_partner(axis, size, digit << low))
            )
        stacked = jnp.stack(pieces)
        acc = stacked[..., :width_acc]
        total = stacked[..., width_acc : width_acc + heads]
        top_each = stacked[..., width_acc + heads :]
        top = jnp.max(top_each, axis=0)
        factor = jnp.exp(top_each - top[None])
        acc = jnp.sum(scale_heads(acc, factor), axis=0)
        total = jnp.sum(total * factor, axis=0)
        packed = jnp.concatenate([acc, total, top], axis=-1)
        low += width
    return packed[0]


def sum_radix(value, axis):
    low = 0
    for width in digit_groups(lax.axis_size(axis)):
        stacked = exchange(value, axis, low, width)
        value = stacked[0]
        for digit in range(1, stacked.shape[0]):
            value = value + stacked[digit]
        low += width
    return value


def local(
    hidden,
    inward_weight,
    output_weight,
    score_gain,
    eigen_rate,
    lengths,
    page_request,
    page_number,
    page_cache,
):
    rows, width_local = hidden.shape
    heads_local = width_local // HEAD_DIM
    gathered = jnp.moveaxis(gather_radix(hidden, "tensor"), 0, 1).reshape(rows, -1)
    projected = jnp.dot(
        gathered,
        inward_weight.reshape(inward_weight.shape[0], -1),
        preferred_element_type=jnp.float32,
    )
    query = head_norm(projected[:, :width_local], score_gain).astype(jnp.bfloat16)
    key_new = head_norm(projected[:, width_local : 2 * width_local], score_gain).astype(
        jnp.bfloat16
    )
    value_own = projected[:, 2 * width_local :].astype(jnp.bfloat16)
    own_score = jnp.sum(
        (query.astype(jnp.float32) * key_new.astype(jnp.float32)).reshape(
            rows, heads_local, HEAD_DIM
        ),
        axis=-1,
    ) / math.sqrt(HEAD_DIM)

    query, page_cache, page_request, page_number, lengths = lax.optimization_barrier(
        (query, page_cache, page_request, page_number, lengths)
    )
    seq_index = lax.axis_index("seq")
    all_queries = gather_xor(query, "seq").reshape(-1, width_local)
    owner_place = ((page_request // rows) ^ seq_index) * rows + page_request % rows
    pages, page_len = (page_cache.shape[0], page_cache.shape[1])
    owner_query = all_queries[owner_place].reshape(pages, heads_local, HEAD_DIM)
    keys_scaled = head_norm(page_cache[:, :, 0, :].astype(jnp.float32), score_gain).astype(
        jnp.bfloat16
    )
    values_paged = page_cache[:, :, 1, :].reshape(pages, page_len, heads_local, HEAD_DIM)
    scores = jnp.einsum(
        "sphd,shd->shp", keys_scaled, owner_query, preferred_element_type=jnp.float32
    ) / math.sqrt(HEAD_DIM)
    positions = page_number[:, None] * page_len + jnp.arange(page_len, dtype=jnp.int32)[None, :]
    live_mask = positions < lengths[page_request][:, None]
    page_max = jnp.max(jnp.where(live_mask[:, None, :], scores, far_below), axis=-1)
    weights = jnp.where(live_mask[:, None, :], jnp.exp(scores - page_max[..., None]), 0.0).astype(
        jnp.bfloat16
    )
    page_total = jnp.sum(weights.astype(jnp.float32), axis=-1)
    page_acc = jnp.einsum(
        "shp,sphd->shd", weights, values_paged, preferred_element_type=jnp.float32
    ).reshape(pages, width_local)

    requests = lengths.shape[0]
    onehot = owner_place[:, None] == jnp.arange(requests, dtype=jnp.int32)[None, :]
    request_max = jnp.max(jnp.where(onehot[:, :, None], page_max[:, None, :], far_below), axis=0)
    factor = jnp.exp(page_max - request_max[owner_place])
    selector = onehot.astype(jnp.float32)
    request_total = jnp.dot(selector.T, page_total * factor, precision=lax.Precision.HIGHEST)
    request_acc = jnp.dot(
        selector.T, scale_heads(page_acc, factor), precision=lax.Precision.HIGHEST
    )
    packed = jnp.concatenate([request_acc, request_total, request_max], axis=1)
    packed = packed.reshape(lax.axis_size("seq"), rows, packed.shape[-1])
    home = scatter_xor(packed, "seq", width_local, heads_local)
    home_acc = home[:, :width_local]
    home_total = home[:, width_local : width_local + heads_local]
    home_max = home[:, width_local + heads_local :]
    final_max = jnp.maximum(home_max, own_score)
    stored_factor = jnp.exp(home_max - final_max)
    total_stored = home_total * stored_factor
    stored = scale_heads(home_acc, stored_factor)
    own_factor = jnp.exp(own_score - final_max)
    total = total_stored + own_factor
    summed = stored + scale_heads(value_own.astype(jnp.float32), own_factor)
    attended = (
        (summed.reshape(rows, heads_local, HEAD_DIM) / total[..., None])
        .reshape(rows, width_local)
        .astype(jnp.bfloat16)
    )
    partial_out = jnp.dot(attended, output_weight, preferred_element_type=jnp.float32)
    attn_out = sum_radix(partial_out, "tensor")
    width = attn_out.shape[1]
    state = gathered.astype(jnp.float32)
    unit = attn_out / jnp.sqrt(jnp.sum(attn_out * attn_out, axis=-1, keepdims=True) / width + epsilon)
    mixed = state + eigen_rate * (unit - state)
    result = mixed / jnp.sqrt(jnp.sum(mixed * mixed, axis=-1, keepdims=True) / width + epsilon)
    first_col = lax.axis_index("tensor") * width_local
    return lax.dynamic_slice_in_dim(result, first_col, width_local, 1).astype(jnp.bfloat16)


def solution(mesh):
    placed = (
        P("seq", "tensor"),
        P(None, None, "tensor"),
        P("tensor", None),
        P("tensor"),
        P(),
        P(),
        P("seq"),
        P("seq"),
        P("seq", None, None, "tensor"),
    )
    return jax.shard_map(
        local, mesh=mesh, in_specs=placed, out_specs=P("seq", "tensor"), check_vma=False
    )
```

```python
import math

import jax
import jax.numpy as jnp
from jax import lax
from jax.sharding import PartitionSpec as P

HEAD_DIM = 64


epsilon = 1e-06
far_below = -1e30


def head_norm(values, gain):
    shaped = values.reshape(values.shape[:-1] + (-1, HEAD_DIM))
    normed = shaped / jnp.sqrt(jnp.mean(shaped * shaped, axis=-1, keepdims=True) + epsilon)
    return normed * gain.reshape(-1, HEAD_DIM)


def scale_heads(summed, factor):
    shaped = summed.reshape(summed.shape[:-1] + (factor.shape[-1], -1))
    return (shaped * factor[..., None]).reshape(summed.shape)


def head_spread(heads, width):
    return (
        jnp.arange(width, dtype=jnp.int32)[None, :] // HEAD_DIM
        == jnp.arange(heads, dtype=jnp.int32)[:, None]
    )


def spread_heads(factor, width):
    spread = head_spread(factor.shape[-1], width).astype(jnp.float32)
    return jnp.dot(factor, spread, precision=lax.Precision.HIGHEST)


def xor_partner(axis, size, bit):
    return [(i, i ^ bit) for i in range(size)]


def digit_groups(size):
    groups = []
    while size > 1:
        width = 2 if size % 4 == 0 else 1
        groups.append(width)
        size >>= width
    return groups


def exchange(held, axis, low, width):
    size = lax.axis_size(axis)
    mine = (lax.axis_index(axis) >> low) & ((1 << width) - 1)
    got = [held] + [
        lax.ppermute(held, axis, perm=xor_partner(axis, size, digit << low))
        for digit in range(1, 1 << width)
    ]
    order = jnp.arange(1 << width, dtype=jnp.int32) ^ mine
    return jnp.take(jnp.stack(got), order, axis=0)


def gather_radix(value, axis):
    held = value[None]
    low = 0
    for width in digit_groups(lax.axis_size(axis)):
        held = exchange(held, axis, low, width).reshape((-1,) + value.shape)
        low += width
    return held


def gather_xor(value, axis):
    size = lax.axis_size(axis)
    held = value[None]
    low = 0
    for width in digit_groups(size):
        got = [held] + [
            lax.ppermute(held, axis, perm=xor_partner(axis, size, digit << low))
            for digit in range(1, 1 << width)
        ]
        held = jnp.stack(got).reshape((-1,) + value.shape)
        low += width
    return held


def scatter_xor(packed, axis, width_acc, heads):
    size = lax.axis_size(axis)
    low = 0
    for width in digit_groups(size):
        count = 1 << width
        grouped = packed.reshape((packed.shape[0] // count, count) + packed.shape[1:])
        pieces = [grouped[:, 0]]
        for digit in range(1, count):
            pieces.append(
                lax.ppermute(grouped[:, digit], axis, perm=xor_partner(axis, size, digit << low))
            )
        stacked = jnp.stack(pieces)
        acc = stacked[..., :width_acc]
        total = stacked[..., width_acc : width_acc + heads]
        top_each = stacked[..., width_acc + heads :]
        top = jnp.max(top_each, axis=0)
        factor = jnp.exp(top_each - top[None])
        acc = jnp.sum(acc * spread_heads(factor, width_acc), axis=0)
        total = jnp.sum(total * factor, axis=0)
        packed = jnp.concatenate([acc, total, top], axis=-1)
        low += width
    return packed[0]


def sum_radix(value, axis):
    low = 0
    for width in digit_groups(lax.axis_size(axis)):
        stacked = exchange(value, axis, low, width)
        value = stacked[0]
        for digit in range(1, stacked.shape[0]):
            value = value + stacked[digit]
        low += width
    return value


def local(
    hidden,
    inward_weight,
    output_weight,
    score_gain,
    eigen_rate,
    lengths,
    page_request,
    page_number,
    page_cache,
):
    rows, width_local = hidden.shape
    heads_local = width_local // HEAD_DIM
    gathered = jnp.moveaxis(gather_radix(hidden, "tensor"), 0, 1).reshape(rows, -1)
    projected = jnp.dot(
        gathered,
        inward_weight.reshape(inward_weight.shape[0], -1),
        preferred_element_type=jnp.float32,
    )
    query = head_norm(projected[:, :width_local], score_gain).astype(jnp.bfloat16)
    key_new = head_norm(projected[:, width_local : 2 * width_local], score_gain).astype(
        jnp.bfloat16
    )
    value_own = projected[:, 2 * width_local :].astype(jnp.bfloat16)
    own_score = jnp.sum(
        (query.astype(jnp.float32) * key_new.astype(jnp.float32)).reshape(
            rows, heads_local, HEAD_DIM
        ),
        axis=-1,
    ) / math.sqrt(HEAD_DIM)

    query, page_cache, page_request, page_number, lengths = lax.optimization_barrier(
        (query, page_cache, page_request, page_number, lengths)
    )
    seq_index = lax.axis_index("seq")
    all_queries = gather_xor(query, "seq").reshape(-1, width_local)
    owner_place = ((page_request // rows) ^ seq_index) * rows + page_request % rows
    pages, page_len = (page_cache.shape[0], page_cache.shape[1])
    owner_query = all_queries[owner_place]
    keys_scaled = head_norm(page_cache[:, :, 0, :].astype(jnp.float32), score_gain).astype(
        jnp.bfloat16
    ).reshape(pages, page_len, width_local)
    values_paged = page_cache[:, :, 1, :]
    spread = head_spread(heads_local, width_local)
    query_blocks = jnp.where(spread.T[None], owner_query[:, :, None], jnp.zeros((), jnp.bfloat16))
    scores = jnp.einsum(
        "spf,sfh->shp", keys_scaled, query_blocks, preferred_element_type=jnp.float32
    ) / math.sqrt(HEAD_DIM)
    positions = page_number[:, None] * page_len + jnp.arange(page_len, dtype=jnp.int32)[None, :]
    live_mask = positions < lengths[page_request][:, None]
    page_max = jnp.max(jnp.where(live_mask[:, None, :], scores, far_below), axis=-1)
    weights = jnp.where(live_mask[:, None, :], jnp.exp(scores - page_max[..., None]), 0.0).astype(
        jnp.bfloat16
    )
    page_total = jnp.sum(weights.astype(jnp.float32), axis=-1)
    acc_blocks = jnp.einsum(
        "shp,spf->shf", weights, values_paged, preferred_element_type=jnp.float32
    )
    page_acc = jnp.sum(jnp.where(spread[None], acc_blocks, 0.0), axis=1)

    requests = lengths.shape[0]
    onehot = owner_place[:, None] == jnp.arange(requests, dtype=jnp.int32)[None, :]
    request_max = jnp.max(jnp.where(onehot[:, :, None], page_max[:, None, :], far_below), axis=0)
    factor = jnp.exp(page_max - request_max[owner_place])
    selector = onehot.astype(jnp.float32)
    request_total = jnp.dot(selector.T, page_total * factor, precision=lax.Precision.HIGHEST)
    request_acc = jnp.dot(
        selector.T, scale_heads(page_acc, factor), precision=lax.Precision.HIGHEST
    )
    packed = jnp.concatenate([request_acc, request_total, request_max], axis=1)
    packed = packed.reshape(lax.axis_size("seq"), rows, packed.shape[-1])
    home = scatter_xor(packed, "seq", width_local, heads_local)
    home_acc = home[:, :width_local]
    home_total = home[:, width_local : width_local + heads_local]
    home_max = home[:, width_local + heads_local :]
    final_max = jnp.maximum(home_max, own_score)
    stored_factor = jnp.exp(home_max - final_max)
    total_stored = home_total * stored_factor
    stored = scale_heads(home_acc, stored_factor)
    own_factor = jnp.exp(own_score - final_max)
    total = total_stored + own_factor
    summed = stored + scale_heads(value_own.astype(jnp.float32), own_factor)
    attended = (
        (summed.reshape(rows, heads_local, HEAD_DIM) / total[..., None])
        .reshape(rows, width_local)
        .astype(jnp.bfloat16)
    )
    partial_out = jnp.dot(attended, output_weight, preferred_element_type=jnp.float32)
    attn_out = sum_radix(partial_out, "tensor")
    width = attn_out.shape[1]
    state = gathered.astype(jnp.float32)
    unit = attn_out / jnp.sqrt(jnp.sum(attn_out * attn_out, axis=-1, keepdims=True) / width + epsilon)
    mixed = state + eigen_rate * (unit - state)
    result = mixed / jnp.sqrt(jnp.sum(mixed * mixed, axis=-1, keepdims=True) / width + epsilon)
    first_col = lax.axis_index("tensor") * width_local
    return lax.dynamic_slice_in_dim(result, first_col, width_local, 1).astype(jnp.bfloat16)


def solution(mesh):
    placed = (
        P("seq", "tensor"),
        P(None, None, "tensor"),
        P("tensor", None),
        P("tensor"),
        P(),
        P(),
        P("seq"),
        P("seq"),
        P("seq", None, None, "tensor"),
    )
    return jax.shard_map(
        local, mesh=mesh, in_specs=placed, out_specs=P("seq", "tensor"), check_vma=False
    )
```

```python
import math

import jax
import jax.numpy as jnp
from jax import lax
from jax.sharding import PartitionSpec as P

HEAD_DIM = 64


epsilon = 1e-06
far_below = -1e30


def head_norm(values, gain):
    shaped = values.reshape(values.shape[:-1] + (-1, HEAD_DIM))
    normed = shaped / jnp.sqrt(jnp.mean(shaped * shaped, axis=-1, keepdims=True) + epsilon)
    return (normed * gain.reshape(-1, HEAD_DIM)).reshape(values.shape)


def scale_heads(summed, factor):
    shaped = summed.reshape(summed.shape[:-1] + (factor.shape[-1], -1))
    return (shaped * factor[..., None]).reshape(summed.shape)


def head_spread(heads, width):
    return (
        jnp.arange(width, dtype=jnp.int32)[None, :] // HEAD_DIM
        == jnp.arange(heads, dtype=jnp.int32)[:, None]
    )


def spread_heads(factor, width):
    spread = head_spread(factor.shape[-1], width).astype(jnp.float32)
    return jnp.dot(factor, spread, precision=lax.Precision.HIGHEST)


def xor_partner(axis, size, bit):
    return [(i, i ^ bit) for i in range(size)]


def digit_groups(size):
    groups = []
    while size > 1:
        width = 2 if size % 4 == 0 else 1
        groups.append(width)
        size >>= width
    return groups


def exchange(held, axis, low, width):
    size = lax.axis_size(axis)
    mine = (lax.axis_index(axis) >> low) & ((1 << width) - 1)
    got = [held] + [
        lax.ppermute(held, axis, perm=xor_partner(axis, size, digit << low))
        for digit in range(1, 1 << width)
    ]
    order = jnp.arange(1 << width, dtype=jnp.int32) ^ mine
    return jnp.take(jnp.stack(got), order, axis=0)


def gather_radix(value, axis):
    held = value[None]
    low = 0
    for width in digit_groups(lax.axis_size(axis)):
        held = exchange(held, axis, low, width).reshape((-1,) + value.shape)
        low += width
    return held


def gather_xor(value, axis):
    size = lax.axis_size(axis)
    held = value[None]
    low = 0
    for width in digit_groups(size):
        got = [held] + [
            lax.ppermute(held, axis, perm=xor_partner(axis, size, digit << low))
            for digit in range(1, 1 << width)
        ]
        held = jnp.stack(got).reshape((-1,) + value.shape)
        low += width
    return held


def scatter_xor(packed, axis, width_acc, heads):
    size = lax.axis_size(axis)
    low = 0
    for width in digit_groups(size):
        count = 1 << width
        grouped = packed.reshape((packed.shape[0] // count, count) + packed.shape[1:])
        pieces = [grouped[:, 0]]
        for digit in range(1, count):
            pieces.append(
                lax.ppermute(grouped[:, digit], axis, perm=xor_partner(axis, size, digit << low))
            )
        stacked = jnp.stack(pieces)
        acc = stacked[..., :width_acc]
        total = stacked[..., width_acc : width_acc + heads]
        top_each = stacked[..., width_acc + heads :]
        top = jnp.max(top_each, axis=0)
        factor = jnp.exp(top_each - top[None])
        acc = jnp.sum(acc * spread_heads(factor, width_acc), axis=0)
        total = jnp.sum(total * factor, axis=0)
        packed = jnp.concatenate([acc, total, top], axis=-1)
        low += width
    return packed[0]


def sum_radix(value, axis):
    low = 0
    for width in digit_groups(lax.axis_size(axis)):
        stacked = exchange(value, axis, low, width)
        value = stacked[0]
        for digit in range(1, stacked.shape[0]):
            value = value + stacked[digit]
        low += width
    return value


def local(
    hidden,
    inward_weight,
    output_weight,
    score_gain,
    eigen_rate,
    lengths,
    page_request,
    page_number,
    page_cache,
):
    rows, width_local = hidden.shape
    heads_local = width_local // HEAD_DIM
    gathered = jnp.moveaxis(gather_radix(hidden, "tensor"), 0, 1).reshape(rows, -1)
    projected = jnp.dot(
        gathered,
        inward_weight.reshape(inward_weight.shape[0], -1),
        preferred_element_type=jnp.float32,
    )
    query = head_norm(projected[:, :width_local], score_gain).astype(jnp.bfloat16)
    key_new = head_norm(projected[:, width_local : 2 * width_local], score_gain).astype(
        jnp.bfloat16
    )
    value_own = projected[:, 2 * width_local :].astype(jnp.bfloat16)
    own_score = jnp.dot(
        query.astype(jnp.float32) * key_new.astype(jnp.float32),
        head_spread(heads_local, width_local).T.astype(jnp.float32),
        precision=lax.Precision.HIGHEST,
    ) / math.sqrt(HEAD_DIM)

    query, page_cache, page_request, page_number, lengths = lax.optimization_barrier(
        (query, page_cache, page_request, page_number, lengths)
    )
    seq_index = lax.axis_index("seq")
    all_queries = gather_xor(query, "seq").reshape(-1, width_local)
    owner_place = ((page_request // rows) ^ seq_index) * rows + page_request % rows
    pages, page_len = (page_cache.shape[0], page_cache.shape[1])
    requests = lengths.shape[0]
    onehot = owner_place[:, None] == jnp.arange(requests, dtype=jnp.int32)[None, :]
    owner_query = jnp.dot(
        onehot.astype(jnp.bfloat16), all_queries, preferred_element_type=jnp.float32
    ).astype(jnp.bfloat16)
    keys_scaled = head_norm(page_cache[:, :, 0, :].astype(jnp.float32), score_gain).astype(
        jnp.bfloat16
    ).reshape(pages, page_len, width_local)
    values_paged = page_cache[:, :, 1, :]
    spread = head_spread(heads_local, width_local)
    query_blocks = jnp.where(spread.T[None], owner_query[:, :, None], jnp.zeros((), jnp.bfloat16))
    scores = jnp.einsum(
        "spf,sfh->shp", keys_scaled, query_blocks, preferred_element_type=jnp.float32
    ) / math.sqrt(HEAD_DIM)
    positions = page_number[:, None] * page_len + jnp.arange(page_len, dtype=jnp.int32)[None, :]
    live_mask = positions < lengths[page_request][:, None]
    page_max = jnp.max(jnp.where(live_mask[:, None, :], scores, far_below), axis=-1)
    weights = jnp.where(live_mask[:, None, :], jnp.exp(scores - page_max[..., None]), 0.0).astype(
        jnp.bfloat16
    )
    page_total = jnp.sum(weights.astype(jnp.float32), axis=-1)
    acc_blocks = jnp.einsum(
        "shp,spf->shf", weights, values_paged, preferred_element_type=jnp.float32
    )
    page_acc = jnp.sum(jnp.where(spread[None], acc_blocks, 0.0), axis=1)

    request_max = jnp.max(jnp.where(onehot[:, :, None], page_max[:, None, :], far_below), axis=0)
    factor = jnp.exp(page_max - request_max[owner_place])
    selector = onehot.astype(jnp.float32)
    request_total = jnp.dot(selector.T, page_total * factor, precision=lax.Precision.HIGHEST)
    request_acc = jnp.dot(
        selector.T, page_acc * spread_heads(factor, width_local), precision=lax.Precision.HIGHEST
    )
    packed = jnp.concatenate([request_acc, request_total, request_max], axis=1)
    packed = packed.reshape(lax.axis_size("seq"), rows, packed.shape[-1])
    home = scatter_xor(packed, "seq", width_local, heads_local)
    home_acc = home[:, :width_local]
    home_total = home[:, width_local : width_local + heads_local]
    home_max = home[:, width_local + heads_local :]
    final_max = jnp.maximum(home_max, own_score)
    stored_factor = jnp.exp(home_max - final_max)
    total_stored = home_total * stored_factor
    stored = home_acc * spread_heads(stored_factor, width_local)
    own_factor = jnp.exp(own_score - final_max)
    total = total_stored + own_factor
    summed = stored + value_own.astype(jnp.float32) * spread_heads(own_factor, width_local)
    attended = (summed / spread_heads(total, width_local)).astype(jnp.bfloat16)
    partial_out = jnp.dot(attended, output_weight, preferred_element_type=jnp.float32)
    attn_out = sum_radix(partial_out, "tensor")
    width = attn_out.shape[1]
    state = gathered.astype(jnp.float32)
    unit = attn_out / jnp.sqrt(jnp.sum(attn_out * attn_out, axis=-1, keepdims=True) / width + epsilon)
    mixed = state + eigen_rate * (unit - state)
    result = mixed / jnp.sqrt(jnp.sum(mixed * mixed, axis=-1, keepdims=True) / width + epsilon)
    first_col = lax.axis_index("tensor") * width_local
    return lax.dynamic_slice_in_dim(result, first_col, width_local, 1).astype(jnp.bfloat16)


def solution(mesh):
    placed = (
        P("seq", "tensor"),
        P(None, None, "tensor"),
        P("tensor", None),
        P("tensor"),
        P(),
        P(),
        P("seq"),
        P("seq"),
        P("seq", None, None, "tensor"),
    )
    return jax.shard_map(
        local, mesh=mesh, in_specs=placed, out_specs=P("seq", "tensor"), check_vma=False
    )
```

```python
import math

import jax
import jax.numpy as jnp
from jax import lax
from jax.sharding import PartitionSpec as P

HEAD_DIM = 64


epsilon = 1e-06
far_below = -1e30


def head_norm(values, gain):
    shaped = values.reshape(values.shape[:-1] + (-1, HEAD_DIM))
    normed = shaped / jnp.sqrt(jnp.mean(shaped * shaped, axis=-1, keepdims=True) + epsilon)
    return (normed * gain.reshape(-1, HEAD_DIM)).reshape(values.shape)


def scale_heads(summed, factor):
    shaped = summed.reshape(summed.shape[:-1] + (factor.shape[-1], -1))
    return (shaped * factor[..., None]).reshape(summed.shape)


def head_spread(heads, width):
    return (
        jnp.arange(width, dtype=jnp.int32)[None, :] // HEAD_DIM
        == jnp.arange(heads, dtype=jnp.int32)[:, None]
    )


def spread_heads(factor, width):
    spread = head_spread(factor.shape[-1], width).astype(jnp.float32)
    return jnp.dot(factor, spread, precision=lax.Precision.HIGHEST)


def xor_partner(axis, size, bit):
    return [(i, i ^ bit) for i in range(size)]


def digit_groups(size):
    groups = []
    while size > 1:
        width = 2 if size % 4 == 0 else 1
        groups.append(width)
        size >>= width
    return groups


def exchange(held, axis, low, width):
    size = lax.axis_size(axis)
    mine = (lax.axis_index(axis) >> low) & ((1 << width) - 1)
    got = [held] + [
        lax.ppermute(held, axis, perm=xor_partner(axis, size, digit << low))
        for digit in range(1, 1 << width)
    ]
    order = jnp.arange(1 << width, dtype=jnp.int32) ^ mine
    return jnp.take(jnp.stack(got), order, axis=0)


def gather_radix(value, axis):
    held = value[None]
    low = 0
    for width in digit_groups(lax.axis_size(axis)):
        held = exchange(held, axis, low, width).reshape((-1,) + value.shape)
        low += width
    return held


def gather_xor(value, axis):
    size = lax.axis_size(axis)
    held = value[None]
    low = 0
    for width in digit_groups(size):
        got = [held] + [
            lax.ppermute(held, axis, perm=xor_partner(axis, size, digit << low))
            for digit in range(1, 1 << width)
        ]
        held = jnp.stack(got).reshape((-1,) + value.shape)
        low += width
    return held


def scatter_xor(packed, axis, width_acc, heads):
    size = lax.axis_size(axis)
    low = 0
    for width in digit_groups(size):
        count = 1 << width
        grouped = packed.reshape((packed.shape[0] // count, count) + packed.shape[1:])
        pieces = [grouped[:, 0]]
        for digit in range(1, count):
            sent = to_link(grouped[:, digit], width_acc, heads)
            pieces.append(
                lax.ppermute(sent, axis, perm=xor_partner(axis, size, digit << low)).astype(
                    jnp.float32
                )
            )
        stacked = jnp.stack(pieces)
        acc = stacked[..., :width_acc]
        total = stacked[..., width_acc : width_acc + heads]
        top_each = stacked[..., width_acc + heads :]
        top = jnp.max(top_each, axis=0)
        factor = jnp.exp(top_each - top[None])
        acc = jnp.sum(acc * spread_heads(factor, width_acc), axis=0)
        total = jnp.sum(total * factor, axis=0)
        packed = jnp.concatenate([acc, total, top], axis=-1)
        low += width
    return packed[0]


def to_link(piece, width_acc, heads):
    top = piece[..., width_acc + heads :]
    top_sent = top.astype(jnp.bfloat16).astype(jnp.float32)
    shift = jnp.exp(jnp.where(top > 0.5 * far_below, top - top_sent, 0.0))
    return jnp.concatenate(
        [
            piece[..., :width_acc] * spread_heads(shift, width_acc),
            piece[..., width_acc : width_acc + heads] * shift,
            top_sent,
        ],
        axis=-1,
    ).astype(jnp.bfloat16)


def sum_radix(value, axis):
    low = 0
    for width in digit_groups(lax.axis_size(axis)):
        stacked = exchange(value, axis, low, width)
        value = stacked[0]
        for digit in range(1, stacked.shape[0]):
            value = value + stacked[digit]
        low += width
    return value


def local(
    hidden,
    inward_weight,
    output_weight,
    score_gain,
    eigen_rate,
    lengths,
    page_request,
    page_number,
    page_cache,
):
    rows, width_local = hidden.shape
    heads_local = width_local // HEAD_DIM
    gathered = jnp.moveaxis(gather_radix(hidden, "tensor"), 0, 1).reshape(rows, -1)
    projected = jnp.dot(
        gathered,
        inward_weight.reshape(inward_weight.shape[0], -1),
        preferred_element_type=jnp.float32,
    )
    query = head_norm(projected[:, :width_local], score_gain).astype(jnp.bfloat16)
    key_new = head_norm(projected[:, width_local : 2 * width_local], score_gain).astype(
        jnp.bfloat16
    )
    value_own = projected[:, 2 * width_local :].astype(jnp.bfloat16)
    own_score = jnp.dot(
        query.astype(jnp.float32) * key_new.astype(jnp.float32),
        head_spread(heads_local, width_local).T.astype(jnp.float32),
        precision=lax.Precision.HIGHEST,
    ) / math.sqrt(HEAD_DIM)

    query, page_cache, page_request, page_number, lengths = lax.optimization_barrier(
        (query, page_cache, page_request, page_number, lengths)
    )
    seq_index = lax.axis_index("seq")
    all_queries = gather_xor(query, "seq").reshape(-1, width_local)
    owner_place = ((page_request // rows) ^ seq_index) * rows + page_request % rows
    pages, page_len = (page_cache.shape[0], page_cache.shape[1])
    requests = lengths.shape[0]
    onehot = owner_place[:, None] == jnp.arange(requests, dtype=jnp.int32)[None, :]
    owner_query = jnp.dot(
        onehot.astype(jnp.bfloat16), all_queries, preferred_element_type=jnp.float32
    ).astype(jnp.bfloat16)
    keys_scaled = head_norm(page_cache[:, :, 0, :].astype(jnp.float32), score_gain).astype(
        jnp.bfloat16
    ).reshape(pages, page_len, width_local)
    values_paged = page_cache[:, :, 1, :]
    spread = head_spread(heads_local, width_local)
    query_blocks = jnp.where(spread.T[None], owner_query[:, :, None], jnp.zeros((), jnp.bfloat16))
    scores = jnp.einsum(
        "spf,sfh->shp", keys_scaled, query_blocks, preferred_element_type=jnp.float32
    ) / math.sqrt(HEAD_DIM)
    positions = page_number[:, None] * page_len + jnp.arange(page_len, dtype=jnp.int32)[None, :]
    live_mask = positions < lengths[page_request][:, None]
    page_max = jnp.max(jnp.where(live_mask[:, None, :], scores, far_below), axis=-1)
    weights = jnp.where(live_mask[:, None, :], jnp.exp(scores - page_max[..., None]), 0.0).astype(
        jnp.bfloat16
    )
    page_total = jnp.sum(weights.astype(jnp.float32), axis=-1)
    acc_blocks = jnp.einsum(
        "shp,spf->shf", weights, values_paged, preferred_element_type=jnp.float32
    )
    page_acc = jnp.sum(jnp.where(spread[None], acc_blocks, 0.0), axis=1)

    request_max = jnp.max(jnp.where(onehot[:, :, None], page_max[:, None, :], far_below), axis=0)
    factor = jnp.exp(page_max - request_max[owner_place])
    selector = (
        jnp.arange(requests, dtype=jnp.int32)[:, None] == owner_place[None, :]
    ).astype(jnp.float32)
    request_total = jnp.dot(selector, page_total * factor, precision=lax.Precision.HIGHEST)
    request_acc = jnp.dot(
        selector, page_acc * spread_heads(factor, width_local), precision=lax.Precision.HIGHEST
    )
    packed = jnp.concatenate([request_acc, request_total, request_max], axis=1)
    packed = packed.reshape(lax.axis_size("seq"), rows, packed.shape[-1])
    home = scatter_xor(packed, "seq", width_local, heads_local)
    home_acc = home[:, :width_local]
    home_total = home[:, width_local : width_local + heads_local]
    home_max = home[:, width_local + heads_local :]
    final_max = jnp.maximum(home_max, own_score)
    stored_factor = jnp.exp(home_max - final_max)
    total_stored = home_total * stored_factor
    stored = home_acc * spread_heads(stored_factor, width_local)
    own_factor = jnp.exp(own_score - final_max)
    total = total_stored + own_factor
    summed = stored + value_own.astype(jnp.float32) * spread_heads(own_factor, width_local)
    attended = (summed / spread_heads(total, width_local)).astype(jnp.bfloat16)
    partial_out = jnp.dot(attended, output_weight, preferred_element_type=jnp.float32)
    attn_out = sum_radix(partial_out, "tensor")
    width = attn_out.shape[1]
    state = gathered.astype(jnp.float32)
    unit = attn_out / jnp.sqrt(jnp.sum(attn_out * attn_out, axis=-1, keepdims=True) / width + epsilon)
    mixed = state + eigen_rate * (unit - state)
    result = mixed / jnp.sqrt(jnp.sum(mixed * mixed, axis=-1, keepdims=True) / width + epsilon)
    first_col = lax.axis_index("tensor") * width_local
    return lax.dynamic_slice_in_dim(result, first_col, width_local, 1).astype(jnp.bfloat16)


def solution(mesh):
    placed = (
        P("seq", "tensor"),
        P(None, None, "tensor"),
        P("tensor", None),
        P("tensor"),
        P(),
        P(),
        P("seq"),
        P("seq"),
        P("seq", None, None, "tensor"),
    )
    return jax.shard_map(
        local, mesh=mesh, in_specs=placed, out_specs=P("seq", "tensor"), check_vma=False
    )
```

```python
import math

import jax
import jax.numpy as jnp
from jax import lax
from jax.sharding import PartitionSpec as P

HEAD_DIM = 64


epsilon = 1e-06
far_below = -1e30


def head_norm(values, gain):
    shaped = values.reshape(values.shape[:-1] + (-1, HEAD_DIM))
    normed = shaped / jnp.sqrt(jnp.mean(shaped * shaped, axis=-1, keepdims=True) + epsilon)
    return (normed * gain.reshape(-1, HEAD_DIM)).reshape(values.shape)


def scale_heads(summed, factor):
    shaped = summed.reshape(summed.shape[:-1] + (factor.shape[-1], -1))
    return (shaped * factor[..., None]).reshape(summed.shape)


def head_spread(heads, width):
    return (
        jnp.arange(width, dtype=jnp.int32)[None, :] // HEAD_DIM
        == jnp.arange(heads, dtype=jnp.int32)[:, None]
    )


def spread_heads(factor, width):
    spread = head_spread(factor.shape[-1], width).astype(jnp.float32)
    return jnp.dot(factor, spread, precision=lax.Precision.HIGHEST)


def xor_partner(axis, size, bit):
    return [(i, i ^ bit) for i in range(size)]


def digit_groups(size):
    groups = []
    while size > 1:
        width = 2 if size % 4 == 0 else 1
        groups.append(width)
        size >>= width
    return groups


def exchange(held, axis, low, width):
    size = lax.axis_size(axis)
    mine = (lax.axis_index(axis) >> low) & ((1 << width) - 1)
    got = [held] + [
        lax.ppermute(held, axis, perm=xor_partner(axis, size, digit << low))
        for digit in range(1, 1 << width)
    ]
    order = jnp.arange(1 << width, dtype=jnp.int32) ^ mine
    return jnp.take(jnp.stack(got), order, axis=0)


def gather_radix(value, axis):
    held = value[None]
    low = 0
    for width in digit_groups(lax.axis_size(axis)):
        held = exchange(held, axis, low, width).reshape((-1,) + value.shape)
        low += width
    return held


def gather_xor(value, axis, riders=(), ride_after=0):
    size = lax.axis_size(axis)
    held = value[None]
    low = 0
    for step, width in enumerate(digit_groups(size)):
        got = [held] + [
            lax.ppermute(held, axis, perm=xor_partner(axis, size, digit << low))
            for digit in range(1, 1 << width)
        ]
        held = jnp.stack(got).reshape((-1,) + value.shape)
        if step == ride_after:
            held, riders = lax.optimization_barrier((held, riders))
        low += width
    return held, riders


def scatter_xor(packed, axis, width_acc, heads):
    size = lax.axis_size(axis)
    low = 0
    for width in digit_groups(size):
        count = 1 << width
        grouped = packed.reshape((packed.shape[0] // count, count) + packed.shape[1:])
        pieces = [grouped[:, 0]]
        for digit in range(1, count):
            sent = to_link(grouped[:, digit], width_acc, heads)
            pieces.append(
                lax.ppermute(sent, axis, perm=xor_partner(axis, size, digit << low)).astype(
                    jnp.float32
                )
            )
        stacked = jnp.stack(pieces)
        acc = stacked[..., :width_acc]
        total = stacked[..., width_acc : width_acc + heads]
        top_each = stacked[..., width_acc + heads :]
        top = jnp.max(top_each, axis=0)
        factor = jnp.exp(top_each - top[None])
        acc = jnp.sum(acc * spread_heads(factor, width_acc), axis=0)
        total = jnp.sum(total * factor, axis=0)
        packed = jnp.concatenate([acc, total, top], axis=-1)
        low += width
    return packed[0]


def to_link(piece, width_acc, heads):
    top = piece[..., width_acc + heads :]
    top_sent = top.astype(jnp.bfloat16).astype(jnp.float32)
    shift = jnp.exp(jnp.where(top > 0.5 * far_below, top - top_sent, 0.0))
    return jnp.concatenate(
        [
            piece[..., :width_acc] * spread_heads(shift, width_acc),
            piece[..., width_acc : width_acc + heads] * shift,
            top_sent,
        ],
        axis=-1,
    ).astype(jnp.bfloat16)


def sum_radix(value, axis):
    size = lax.axis_size(axis)
    low = 0
    for width in digit_groups(size):
        got = [value] + [
            lax.ppermute(value, axis, perm=xor_partner(axis, size, digit << low))
            for digit in range(1, 1 << width)
        ]
        while len(got) > 1:
            got = [got[i] + got[i + 1] for i in range(0, len(got), 2)]
        value = got[0]
        low += width
    return value


def local(
    hidden,
    inward_weight,
    output_weight,
    score_gain,
    eigen_rate,
    lengths,
    page_request,
    page_number,
    page_cache,
):
    rows, width_local = hidden.shape
    heads_local = width_local // HEAD_DIM
    gathered = jnp.moveaxis(gather_radix(hidden, "tensor"), 0, 1).reshape(rows, -1)
    projected = jnp.dot(
        gathered,
        inward_weight.reshape(inward_weight.shape[0], -1),
        preferred_element_type=jnp.float32,
    )
    query = head_norm(projected[:, :width_local], score_gain).astype(jnp.bfloat16)
    key_new = head_norm(projected[:, width_local : 2 * width_local], score_gain).astype(
        jnp.bfloat16
    )
    value_own = projected[:, 2 * width_local :].astype(jnp.bfloat16)
    own_score = jnp.dot(
        query.astype(jnp.float32) * key_new.astype(jnp.float32),
        head_spread(heads_local, width_local).T.astype(jnp.float32),
        precision=lax.Precision.HIGHEST,
    ) / math.sqrt(HEAD_DIM)

    seq_index = lax.axis_index("seq")
    all_queries, (page_cache, page_request, page_number, lengths) = gather_xor(
        query, "seq", (page_cache, page_request, page_number, lengths), 0
    )
    all_queries = all_queries.reshape(-1, width_local)
    owner_place = ((page_request // rows) ^ seq_index) * rows + page_request % rows
    pages, page_len = (page_cache.shape[0], page_cache.shape[1])
    requests = lengths.shape[0]
    onehot = owner_place[:, None] == jnp.arange(requests, dtype=jnp.int32)[None, :]
    owner_query = jnp.dot(
        onehot.astype(jnp.bfloat16), all_queries, preferred_element_type=jnp.float32
    ).astype(jnp.bfloat16)
    keys_scaled = head_norm(page_cache[:, :, 0, :].astype(jnp.float32), score_gain).astype(
        jnp.bfloat16
    ).reshape(pages, page_len, width_local)
    values_paged = page_cache[:, :, 1, :]
    spread = head_spread(heads_local, width_local)
    query_blocks = jnp.where(spread.T[None], owner_query[:, :, None], jnp.zeros((), jnp.bfloat16))
    scores = jnp.einsum(
        "spf,sfh->shp", keys_scaled, query_blocks, preferred_element_type=jnp.float32
    ) / math.sqrt(HEAD_DIM)
    positions = page_number[:, None] * page_len + jnp.arange(page_len, dtype=jnp.int32)[None, :]
    live_mask = positions < lengths[page_request][:, None]
    page_max = jnp.max(jnp.where(live_mask[:, None, :], scores, far_below), axis=-1)
    weights = jnp.where(live_mask[:, None, :], jnp.exp(scores - page_max[..., None]), 0.0).astype(
        jnp.bfloat16
    )
    page_total = jnp.sum(weights.astype(jnp.float32), axis=-1)
    acc_blocks = jnp.einsum(
        "shp,spf->shf", weights, values_paged, preferred_element_type=jnp.float32
    )
    page_acc = jnp.sum(jnp.where(spread[None], acc_blocks, 0.0), axis=1)

    chosen = jnp.arange(requests, dtype=jnp.int32)[:, None] == owner_place[None, :]
    request_max = jnp.max(jnp.where(chosen[:, :, None], page_max[None, :, :], far_below), axis=1)
    factor = jnp.exp(page_max - request_max[owner_place])
    selector = chosen.astype(jnp.float32)
    request_total = jnp.dot(selector, page_total * factor, precision=lax.Precision.HIGHEST)
    request_acc = jnp.dot(
        selector, page_acc * spread_heads(factor, width_local), precision=lax.Precision.HIGHEST
    )
    packed = jnp.concatenate([request_acc, request_total, request_max], axis=1)
    packed = packed.reshape(lax.axis_size("seq"), rows, packed.shape[-1])
    home = scatter_xor(packed, "seq", width_local, heads_local)
    home_acc = home[:, :width_local]
    home_total = home[:, width_local : width_local + heads_local]
    home_max = home[:, width_local + heads_local :]
    final_max = jnp.maximum(home_max, own_score)
    stored_factor = jnp.exp(home_max - final_max)
    total_stored = home_total * stored_factor
    stored = home_acc * spread_heads(stored_factor, width_local)
    own_factor = jnp.exp(own_score - final_max)
    total = total_stored + own_factor
    summed = stored + value_own.astype(jnp.float32) * spread_heads(own_factor, width_local)
    attended = (summed / spread_heads(total, width_local)).astype(jnp.bfloat16)
    partial_out = jnp.dot(attended, output_weight, preferred_element_type=jnp.float32)
    attn_out = sum_radix(partial_out, "tensor")
    width = attn_out.shape[1]
    state = gathered.astype(jnp.float32)
    unit = attn_out / jnp.sqrt(jnp.sum(attn_out * attn_out, axis=-1, keepdims=True) / width + epsilon)
    mixed = state + eigen_rate * (unit - state)
    result = mixed / jnp.sqrt(jnp.sum(mixed * mixed, axis=-1, keepdims=True) / width + epsilon)
    first_col = lax.axis_index("tensor") * width_local
    return lax.dynamic_slice_in_dim(result, first_col, width_local, 1).astype(jnp.bfloat16)


def solution(mesh):
    placed = (
        P("seq", "tensor"),
        P(None, None, "tensor"),
        P("tensor", None),
        P("tensor"),
        P(),
        P(),
        P("seq"),
        P("seq"),
        P("seq", None, None, "tensor"),
    )
    return jax.shard_map(
        local, mesh=mesh, in_specs=placed, out_specs=P("seq", "tensor"), check_vma=False
    )
```

```python
import math

import jax
import jax.numpy as jnp
from jax import lax
from jax.sharding import PartitionSpec as P

HEAD_DIM = 64


epsilon = 1e-06
far_below = -1e30


def head_norm(values, gain):
    shaped = values.reshape(values.shape[:-1] + (-1, HEAD_DIM))
    normed = shaped / jnp.sqrt(jnp.mean(shaped * shaped, axis=-1, keepdims=True) + epsilon)
    return (normed * gain.reshape(-1, HEAD_DIM)).reshape(values.shape)


def scale_heads(summed, factor):
    shaped = summed.reshape(summed.shape[:-1] + (factor.shape[-1], -1))
    return (shaped * factor[..., None]).reshape(summed.shape)


def head_spread(heads, width):
    return (
        jnp.arange(width, dtype=jnp.int32)[None, :] // HEAD_DIM
        == jnp.arange(heads, dtype=jnp.int32)[:, None]
    )


def spread_heads(factor, width):
    spread = head_spread(factor.shape[-1], width).astype(jnp.float32)
    return jnp.dot(factor, spread, precision=lax.Precision.HIGHEST)


def xor_partner(axis, size, bit):
    return [(i, i ^ bit) for i in range(size)]


def digit_groups(size):
    groups = []
    while size > 1:
        width = 2 if size % 4 == 0 else 1
        groups.append(width)
        size >>= width
    return groups


def exchange(held, axis, low, width):
    size = lax.axis_size(axis)
    mine = (lax.axis_index(axis) >> low) & ((1 << width) - 1)
    got = [held] + [
        lax.ppermute(held, axis, perm=xor_partner(axis, size, digit << low))
        for digit in range(1, 1 << width)
    ]
    order = jnp.arange(1 << width, dtype=jnp.int32) ^ mine
    return jnp.take(jnp.stack(got), order, axis=0)


def gather_radix(value, axis):
    held = value[None]
    low = 0
    for width in digit_groups(lax.axis_size(axis)):
        held = exchange(held, axis, low, width).reshape((-1,) + value.shape)
        low += width
    return held


def gather_xor(value, axis, riders=(), ride_after=0):
    size = lax.axis_size(axis)
    held = value[None]
    low = 0
    for step, width in enumerate(digit_groups(size)):
        got = [held] + [
            lax.ppermute(held, axis, perm=xor_partner(axis, size, digit << low))
            for digit in range(1, 1 << width)
        ]
        held = jnp.stack(got).reshape((-1,) + value.shape)
        if step == ride_after:
            held, riders = lax.optimization_barrier((held, riders))
        low += width
    return held, riders


def scatter_xor(packed, axis, width_acc, heads):
    size = lax.axis_size(axis)
    low = 0
    for width in digit_groups(size):
        count = 1 << width
        grouped = packed.reshape((packed.shape[0] // count, count) + packed.shape[1:])
        pieces = [grouped[:, 0]]
        for digit in range(1, count):
            sent = to_link(grouped[:, digit], width_acc, heads)
            pieces.append(
                lax.ppermute(sent, axis, perm=xor_partner(axis, size, digit << low)).astype(
                    jnp.float32
                )
            )
        stacked = jnp.stack(pieces)
        acc = stacked[..., :width_acc]
        total = stacked[..., width_acc : width_acc + heads]
        top_each = stacked[..., width_acc + heads :]
        top = jnp.max(top_each, axis=0)
        factor = jnp.exp(top_each - top[None])
        acc = jnp.sum(acc * spread_heads(factor, width_acc), axis=0)
        total = jnp.sum(total * factor, axis=0)
        packed = jnp.concatenate([acc, total, top], axis=-1)
        low += width
    return packed[0]


def to_link(piece, width_acc, heads):
    top = piece[..., width_acc + heads :]
    top_sent = top.astype(jnp.bfloat16).astype(jnp.float32)
    shift = jnp.exp(jnp.where(top > 0.5 * far_below, top - top_sent, 0.0))
    return jnp.concatenate(
        [
            piece[..., :width_acc] * spread_heads(shift, width_acc),
            piece[..., width_acc : width_acc + heads] * shift,
            top_sent,
        ],
        axis=-1,
    ).astype(jnp.bfloat16)


def sum_radix(value, axis):
    size = lax.axis_size(axis)
    low = 0
    for width in digit_groups(size):
        got = [value] + [
            lax.ppermute(value, axis, perm=xor_partner(axis, size, digit << low))
            for digit in range(1, 1 << width)
        ]
        while len(got) > 1:
            got = [got[i] + got[i + 1] for i in range(0, len(got), 2)]
        value = got[0]
        low += width
    return value


def local(
    hidden,
    inward_weight,
    output_weight,
    score_gain,
    eigen_rate,
    lengths,
    page_request,
    page_number,
    page_cache,
):
    rows, width_local = hidden.shape
    heads_local = width_local // HEAD_DIM
    gathered = jnp.moveaxis(gather_radix(hidden, "tensor"), 0, 1).reshape(rows, -1)
    projected = jnp.dot(
        gathered,
        inward_weight.reshape(inward_weight.shape[0], -1),
        preferred_element_type=jnp.float32,
    )
    query = head_norm(projected[:, :width_local], score_gain).astype(jnp.bfloat16)
    key_new = head_norm(projected[:, width_local : 2 * width_local], score_gain).astype(
        jnp.bfloat16
    )
    value_own = projected[:, 2 * width_local :].astype(jnp.bfloat16)
    own_score = jnp.dot(
        query.astype(jnp.float32) * key_new.astype(jnp.float32),
        head_spread(heads_local, width_local).T.astype(jnp.float32),
        precision=lax.Precision.HIGHEST,
    ) / math.sqrt(HEAD_DIM)

    seq_index = lax.axis_index("seq")
    query, page_cache, page_request, page_number, lengths = lax.optimization_barrier(
        (query, page_cache, page_request, page_number, lengths)
    )
    all_queries, _ = gather_xor(query, "seq")
    all_queries = all_queries.reshape(-1, width_local)
    owner_place = ((page_request // rows) ^ seq_index) * rows + page_request % rows
    pages, page_len = (page_cache.shape[0], page_cache.shape[1])
    requests = lengths.shape[0]
    onehot = owner_place[:, None] == jnp.arange(requests, dtype=jnp.int32)[None, :]
    owner_query = jnp.dot(
        onehot.astype(jnp.bfloat16), all_queries, preferred_element_type=jnp.float32
    ).astype(jnp.bfloat16)
    keys_scaled = head_norm(page_cache[:, :, 0, :].astype(jnp.float32), score_gain).astype(
        jnp.bfloat16
    ).reshape(pages, page_len, width_local)
    values_paged = page_cache[:, :, 1, :]
    spread = head_spread(heads_local, width_local)
    query_blocks = jnp.where(spread.T[None], owner_query[:, :, None], jnp.zeros((), jnp.bfloat16))
    scores = jnp.einsum(
        "spf,sfh->shp", keys_scaled, query_blocks, preferred_element_type=jnp.float32
    ) / math.sqrt(HEAD_DIM)
    positions = page_number[:, None] * page_len + jnp.arange(page_len, dtype=jnp.int32)[None, :]
    live_mask = positions < lengths[page_request][:, None]
    page_max = jnp.max(jnp.where(live_mask[:, None, :], scores, far_below), axis=-1)
    weights = jnp.where(live_mask[:, None, :], jnp.exp(scores - page_max[..., None]), 0.0).astype(
        jnp.bfloat16
    )
    page_total = jnp.sum(weights.astype(jnp.float32), axis=-1)
    acc_blocks = jnp.einsum(
        "shp,spf->shf", weights, values_paged, preferred_element_type=jnp.float32
    )
    page_acc = jnp.sum(jnp.where(spread[None], acc_blocks, 0.0), axis=1)

    chosen = jnp.arange(requests, dtype=jnp.int32)[:, None] == owner_place[None, :]
    request_max = jnp.max(jnp.where(chosen[:, :, None], page_max[None, :, :], far_below), axis=1)
    factor = jnp.exp(page_max - request_max[owner_place])
    selector = chosen.astype(jnp.float32)
    request_total = jnp.dot(selector, page_total * factor, precision=lax.Precision.HIGHEST)
    request_acc = jnp.dot(
        selector, page_acc * spread_heads(factor, width_local), precision=lax.Precision.HIGHEST
    )
    packed = jnp.concatenate([request_acc, request_total, request_max], axis=1)
    packed = packed.reshape(lax.axis_size("seq"), rows, packed.shape[-1])
    home = scatter_xor(packed, "seq", width_local, heads_local)
    home_acc = home[:, :width_local]
    home_total = home[:, width_local : width_local + heads_local]
    home_max = home[:, width_local + heads_local :]
    final_max = jnp.maximum(home_max, own_score)
    stored_factor = jnp.exp(home_max - final_max)
    total_stored = home_total * stored_factor
    stored = home_acc * spread_heads(stored_factor, width_local)
    own_factor = jnp.exp(own_score - final_max)
    total = total_stored + own_factor
    summed = stored + value_own.astype(jnp.float32) * spread_heads(own_factor, width_local)
    attended = (summed / spread_heads(total, width_local)).astype(jnp.bfloat16)
    partial_out = jnp.dot(attended, output_weight, preferred_element_type=jnp.float32)
    attn_out = sum_radix(partial_out, "tensor")
    width = attn_out.shape[1]
    state = gathered.astype(jnp.float32)
    unit = attn_out / jnp.sqrt(jnp.sum(attn_out * attn_out, axis=-1, keepdims=True) / width + epsilon)
    mixed = state + eigen_rate * (unit - state)
    result = mixed / jnp.sqrt(jnp.sum(mixed * mixed, axis=-1, keepdims=True) / width + epsilon)
    first_col = lax.axis_index("tensor") * width_local
    return lax.dynamic_slice_in_dim(result, first_col, width_local, 1).astype(jnp.bfloat16)


def solution(mesh):
    placed = (
        P("seq", "tensor"),
        P(None, None, "tensor"),
        P("tensor", None),
        P("tensor"),
        P(),
        P(),
        P("seq"),
        P("seq"),
        P("seq", None, None, "tensor"),
    )
    return jax.shard_map(
        local, mesh=mesh, in_specs=placed, out_specs=P("seq", "tensor"), check_vma=False
    )
```

```python
import math

import jax
import jax.numpy as jnp
from jax import lax
from jax.sharding import PartitionSpec as P

HEAD_DIM = 64


epsilon = 1e-06
far_below = -1e30


def head_norm(values, gain):
    shaped = values.reshape(values.shape[:-1] + (-1, HEAD_DIM))
    normed = shaped / jnp.sqrt(jnp.mean(shaped * shaped, axis=-1, keepdims=True) + epsilon)
    return (normed * gain.reshape(-1, HEAD_DIM)).reshape(values.shape)


def scale_heads(summed, factor):
    shaped = summed.reshape(summed.shape[:-1] + (factor.shape[-1], -1))
    return (shaped * factor[..., None]).reshape(summed.shape)


def head_spread(heads, width):
    return (
        jnp.arange(width, dtype=jnp.int32)[None, :] // HEAD_DIM
        == jnp.arange(heads, dtype=jnp.int32)[:, None]
    )


def spread_heads(factor, width):
    spread = head_spread(factor.shape[-1], width).astype(jnp.float32)
    return jnp.dot(factor, spread, precision=lax.Precision.HIGHEST)


def xor_partner(axis, size, bit):
    return [(i, i ^ bit) for i in range(size)]


def digit_groups(size):
    groups = []
    while size > 1:
        width = 2 if size % 4 == 0 else 1
        groups.append(width)
        size >>= width
    return groups


def exchange(held, axis, low, width):
    size = lax.axis_size(axis)
    mine = (lax.axis_index(axis) >> low) & ((1 << width) - 1)
    got = [held] + [
        lax.ppermute(held, axis, perm=xor_partner(axis, size, digit << low))
        for digit in range(1, 1 << width)
    ]
    order = jnp.arange(1 << width, dtype=jnp.int32) ^ mine
    return jnp.take(jnp.stack(got), order, axis=0)


def gather_radix(value, axis):
    held = value[None]
    low = 0
    for width in digit_groups(lax.axis_size(axis)):
        held = exchange(held, axis, low, width).reshape((-1,) + value.shape)
        low += width
    return held


def gather_xor(value, axis, riders=(), ride_after=0):
    size = lax.axis_size(axis)
    held = value[None]
    low = 0
    for step, width in enumerate(digit_groups(size)):
        got = [held] + [
            lax.ppermute(held, axis, perm=xor_partner(axis, size, digit << low))
            for digit in range(1, 1 << width)
        ]
        held = jnp.stack(got).reshape((-1,) + value.shape)
        if step == ride_after:
            held, riders = lax.optimization_barrier((held, riders))
        low += width
    return held, riders


def scatter_xor(packed, axis, width_acc, heads):
    size = lax.axis_size(axis)
    low = 0
    for width in digit_groups(size):
        count = 1 << width
        grouped = packed.reshape((packed.shape[0] // count, count) + packed.shape[1:])
        pieces = [grouped[:, 0]]
        for digit in range(1, count):
            sent = to_link(grouped[:, digit], width_acc, heads)
            pieces.append(
                lax.ppermute(sent, axis, perm=xor_partner(axis, size, digit << low)).astype(
                    jnp.float32
                )
            )
        stacked = jnp.stack(pieces)
        acc = stacked[..., :width_acc]
        total = stacked[..., width_acc : width_acc + heads]
        top_each = stacked[..., width_acc + heads :]
        top = jnp.max(top_each, axis=0)
        factor = jnp.exp(top_each - top[None])
        acc = jnp.sum(acc * spread_heads(factor, width_acc), axis=0)
        total = jnp.sum(total * factor, axis=0)
        packed = jnp.concatenate([acc, total, top], axis=-1)
        low += width
    return packed[0]


def to_link(piece, width_acc, heads):
    top = piece[..., width_acc + heads :]
    top_sent = top.astype(jnp.bfloat16).astype(jnp.float32)
    shift = jnp.exp(jnp.where(top > 0.5 * far_below, top - top_sent, 0.0))
    return jnp.concatenate(
        [
            piece[..., :width_acc] * spread_heads(shift, width_acc),
            piece[..., width_acc : width_acc + heads] * shift,
            top_sent,
        ],
        axis=-1,
    ).astype(jnp.bfloat16)


def sum_radix(value, axis):
    size = lax.axis_size(axis)
    low = 0
    for width in digit_groups(size):
        sent = value.astype(jnp.bfloat16)
        got = [value] + [
            lax.ppermute(sent, axis, perm=xor_partner(axis, size, digit << low)).astype(value.dtype)
            for digit in range(1, 1 << width)
        ]
        while len(got) > 1:
            got = [got[i] + got[i + 1] for i in range(0, len(got), 2)]
        value = got[0]
        low += width
    return value


def local(
    hidden,
    inward_weight,
    output_weight,
    score_gain,
    eigen_rate,
    lengths,
    page_request,
    page_number,
    page_cache,
):
    rows, width_local = hidden.shape
    heads_local = width_local // HEAD_DIM
    gathered = jnp.moveaxis(gather_radix(hidden, "tensor"), 0, 1).reshape(rows, -1)
    projected = jnp.dot(
        gathered,
        inward_weight.reshape(inward_weight.shape[0], -1),
        preferred_element_type=jnp.float32,
    )
    query = head_norm(projected[:, :width_local], score_gain).astype(jnp.bfloat16)
    key_new = head_norm(projected[:, width_local : 2 * width_local], score_gain).astype(
        jnp.bfloat16
    )
    value_own = projected[:, 2 * width_local :].astype(jnp.bfloat16)
    own_score = jnp.dot(
        query.astype(jnp.float32) * key_new.astype(jnp.float32),
        head_spread(heads_local, width_local).T.astype(jnp.float32),
        precision=lax.Precision.HIGHEST,
    ) / math.sqrt(HEAD_DIM)

    seq_index = lax.axis_index("seq")
    query, page_cache, page_request, page_number, lengths = lax.optimization_barrier(
        (query, page_cache, page_request, page_number, lengths)
    )
    all_queries, _ = gather_xor(query, "seq")
    all_queries = all_queries.reshape(-1, width_local)
    owner_place = ((page_request // rows) ^ seq_index) * rows + page_request % rows
    pages, page_len = (page_cache.shape[0], page_cache.shape[1])
    requests = lengths.shape[0]
    onehot = owner_place[:, None] == jnp.arange(requests, dtype=jnp.int32)[None, :]
    owner_query = jnp.dot(
        onehot.astype(jnp.bfloat16), all_queries, preferred_element_type=jnp.float32
    ).astype(jnp.bfloat16)
    keys_scaled = head_norm(page_cache[:, :, 0, :].astype(jnp.float32), score_gain).astype(
        jnp.bfloat16
    ).reshape(pages, page_len, width_local)
    values_paged = page_cache[:, :, 1, :]
    spread = head_spread(heads_local, width_local)
    query_blocks = jnp.where(spread.T[None], owner_query[:, :, None], jnp.zeros((), jnp.bfloat16))
    scores = jnp.einsum(
        "spf,sfh->shp", keys_scaled, query_blocks, preferred_element_type=jnp.float32
    ) / math.sqrt(HEAD_DIM)
    positions = page_number[:, None] * page_len + jnp.arange(page_len, dtype=jnp.int32)[None, :]
    live_mask = positions < lengths[page_request][:, None]
    page_max = jnp.max(jnp.where(live_mask[:, None, :], scores, far_below), axis=-1)
    weights = jnp.where(live_mask[:, None, :], jnp.exp(scores - page_max[..., None]), 0.0).astype(
        jnp.bfloat16
    )
    page_total = jnp.sum(weights.astype(jnp.float32), axis=-1)
    acc_blocks = jnp.einsum(
        "shp,spf->shf", weights, values_paged, preferred_element_type=jnp.float32
    )
    page_acc = jnp.sum(jnp.where(spread[None], acc_blocks, 0.0), axis=1)

    chosen = jnp.arange(requests, dtype=jnp.int32)[:, None] == owner_place[None, :]
    request_max = jnp.max(jnp.where(chosen[:, :, None], page_max[None, :, :], far_below), axis=1)
    factor = jnp.exp(page_max - request_max[owner_place])
    selector = chosen.astype(jnp.float32)
    request_total = jnp.dot(selector, page_total * factor, precision=lax.Precision.HIGHEST)
    request_acc = jnp.dot(
        selector, page_acc * spread_heads(factor, width_local), precision=lax.Precision.HIGHEST
    )
    packed = jnp.concatenate([request_acc, request_total, request_max], axis=1)
    packed = packed.reshape(lax.axis_size("seq"), rows, packed.shape[-1])
    home = scatter_xor(packed, "seq", width_local, heads_local)
    home_acc = home[:, :width_local]
    home_total = home[:, width_local : width_local + heads_local]
    home_max = home[:, width_local + heads_local :]
    final_max = jnp.maximum(home_max, own_score)
    stored_factor = jnp.exp(home_max - final_max)
    total_stored = home_total * stored_factor
    stored = home_acc * spread_heads(stored_factor, width_local)
    own_factor = jnp.exp(own_score - final_max)
    total = total_stored + own_factor
    summed = stored + value_own.astype(jnp.float32) * spread_heads(own_factor, width_local)
    attended = (summed / spread_heads(total, width_local)).astype(jnp.bfloat16)
    partial_out = jnp.dot(attended, output_weight, preferred_element_type=jnp.float32)
    attn_out = sum_radix(partial_out, "tensor")
    width = attn_out.shape[1]
    state = gathered.astype(jnp.float32)
    unit = attn_out / jnp.sqrt(jnp.sum(attn_out * attn_out, axis=-1, keepdims=True) / width + epsilon)
    mixed = state + eigen_rate * (unit - state)
    result = mixed / jnp.sqrt(jnp.sum(mixed * mixed, axis=-1, keepdims=True) / width + epsilon)
    first_col = lax.axis_index("tensor") * width_local
    return lax.dynamic_slice_in_dim(result, first_col, width_local, 1).astype(jnp.bfloat16)


def solution(mesh):
    placed = (
        P("seq", "tensor"),
        P(None, None, "tensor"),
        P("tensor", None),
        P("tensor"),
        P(),
        P(),
        P("seq"),
        P("seq"),
        P("seq", None, None, "tensor"),
    )
    return jax.shard_map(
        local, mesh=mesh, in_specs=placed, out_specs=P("seq", "tensor"), check_vma=False
    )
```

```python
import math

import jax
import jax.numpy as jnp
from jax import lax
from jax.sharding import PartitionSpec as P

HEAD_DIM = 64


epsilon = 1e-06
far_below = -1e30


def head_norm(values, gain):
    shaped = values.reshape(values.shape[:-1] + (-1, HEAD_DIM))
    normed = shaped / jnp.sqrt(jnp.mean(shaped * shaped, axis=-1, keepdims=True) + epsilon)
    return (normed * gain.reshape(-1, HEAD_DIM)).reshape(values.shape)


def scale_heads(summed, factor):
    shaped = summed.reshape(summed.shape[:-1] + (factor.shape[-1], -1))
    return (shaped * factor[..., None]).reshape(summed.shape)


def head_spread(heads, width):
    return (
        jnp.arange(width, dtype=jnp.int32)[None, :] // HEAD_DIM
        == jnp.arange(heads, dtype=jnp.int32)[:, None]
    )


def spread_heads(factor, width):
    spread = head_spread(factor.shape[-1], width).astype(jnp.float32)
    return jnp.dot(factor, spread, precision=lax.Precision.HIGHEST)


def xor_partner(axis, size, bit):
    return [(i, i ^ bit) for i in range(size)]


def digit_groups(size):
    groups = []
    while size > 1:
        width = 2 if size % 4 == 0 else 1
        groups.append(width)
        size >>= width
    return groups


def exchange(held, axis, low, width):
    size = lax.axis_size(axis)
    mine = (lax.axis_index(axis) >> low) & ((1 << width) - 1)
    got = [held] + [
        lax.ppermute(held, axis, perm=xor_partner(axis, size, digit << low))
        for digit in range(1, 1 << width)
    ]
    order = jnp.arange(1 << width, dtype=jnp.int32) ^ mine
    return jnp.take(jnp.stack(got), order, axis=0)


def gather_radix(value, axis):
    held = value[None]
    low = 0
    for width in digit_groups(lax.axis_size(axis)):
        held = exchange(held, axis, low, width).reshape((-1,) + value.shape)
        low += width
    return held


def gather_xor(value, axis, riders=(), ride_after=0):
    size = lax.axis_size(axis)
    held = value[None]
    low = 0
    for step, width in enumerate(digit_groups(size)):
        got = [held] + [
            lax.ppermute(held, axis, perm=xor_partner(axis, size, digit << low))
            for digit in range(1, 1 << width)
        ]
        held = jnp.stack(got).reshape((-1,) + value.shape)
        if step == ride_after:
            held, riders = lax.optimization_barrier((held, riders))
        low += width
    return held, riders


def scatter_xor(packed, axis, width_acc, heads):
    size = lax.axis_size(axis)
    low = 0
    for width in digit_groups(size):
        count = 1 << width
        grouped = packed.reshape((packed.shape[0] // count, count) + packed.shape[1:])
        pieces = [grouped[:, 0]]
        for digit in range(1, count):
            sent = to_link(grouped[:, digit], width_acc, heads)
            pieces.append(
                lax.ppermute(sent, axis, perm=xor_partner(axis, size, digit << low)).astype(
                    jnp.float32
                )
            )
        stacked = jnp.stack(pieces)
        acc = stacked[..., :width_acc]
        total = stacked[..., width_acc : width_acc + heads]
        top_each = stacked[..., width_acc + heads :]
        top = jnp.max(top_each, axis=0)
        factor = jnp.exp(top_each - top[None])
        acc = jnp.sum(acc * spread_heads(factor, width_acc), axis=0)
        total = jnp.sum(total * factor, axis=0)
        packed = jnp.concatenate([acc, total, top], axis=-1)
        low += width
    return packed[0]


def to_link(piece, width_acc, heads):
    top = piece[..., width_acc + heads :]
    top_sent = top.astype(jnp.bfloat16).astype(jnp.float32)
    shift = jnp.exp(jnp.where(top > 0.5 * far_below, top - top_sent, 0.0))
    return jnp.concatenate(
        [
            piece[..., :width_acc] * spread_heads(shift, width_acc),
            piece[..., width_acc : width_acc + heads] * shift,
            top_sent,
        ],
        axis=-1,
    ).astype(jnp.bfloat16)


def sum_radix(value, axis):
    size = lax.axis_size(axis)
    low = 0
    for width in digit_groups(size):
        sent = value.astype(jnp.bfloat16)
        got = [value] + [
            lax.ppermute(sent, axis, perm=xor_partner(axis, size, digit << low)).astype(value.dtype)
            for digit in range(1, 1 << width)
        ]
        while len(got) > 1:
            got = [got[i] + got[i + 1] for i in range(0, len(got), 2)]
        value = got[0]
        low += width
    return value


def local(
    hidden,
    inward_weight,
    output_weight,
    score_gain,
    eigen_rate,
    lengths,
    page_request,
    page_number,
    page_cache,
):
    rows, width_local = hidden.shape
    heads_local = width_local // HEAD_DIM
    gathered = jnp.moveaxis(gather_radix(hidden, "tensor"), 0, 1).reshape(rows, -1)
    projected = jnp.dot(
        gathered,
        inward_weight.reshape(inward_weight.shape[0], -1),
        preferred_element_type=jnp.float32,
    )
    query = head_norm(projected[:, :width_local], score_gain).astype(jnp.bfloat16)
    key_new = head_norm(projected[:, width_local : 2 * width_local], score_gain).astype(
        jnp.bfloat16
    )
    value_own = projected[:, 2 * width_local :].astype(jnp.bfloat16)
    own_score = jnp.dot(
        query.astype(jnp.float32) * key_new.astype(jnp.float32),
        head_spread(heads_local, width_local).T.astype(jnp.float32),
        precision=lax.Precision.HIGHEST,
    ) / math.sqrt(HEAD_DIM)

    seq_index = lax.axis_index("seq")
    query, page_cache, page_request, page_number, lengths = lax.optimization_barrier(
        (query, page_cache, page_request, page_number, lengths)
    )
    all_queries, _ = gather_xor(query, "seq", (), -1)
    all_queries = all_queries.reshape(-1, width_local)
    owner_place = ((page_request // rows) ^ seq_index) * rows + page_request % rows
    pages, page_len = (page_cache.shape[0], page_cache.shape[1])
    requests = lengths.shape[0]
    onehot = owner_place[:, None] == jnp.arange(requests, dtype=jnp.int32)[None, :]
    owner_query = jnp.dot(
        onehot.astype(jnp.bfloat16), all_queries, preferred_element_type=jnp.float32
    ).astype(jnp.bfloat16)
    keys_scaled = head_norm(page_cache[:, :, 0, :].astype(jnp.float32), score_gain).astype(
        jnp.bfloat16
    ).reshape(pages, page_len, width_local)
    values_paged = page_cache[:, :, 1, :]
    spread = head_spread(heads_local, width_local)
    query_blocks = jnp.where(spread.T[None], owner_query[:, :, None], jnp.zeros((), jnp.bfloat16))
    scores = jnp.einsum(
        "spf,sfh->shp", keys_scaled, query_blocks, preferred_element_type=jnp.float32
    ) / math.sqrt(HEAD_DIM)
    positions = page_number[:, None] * page_len + jnp.arange(page_len, dtype=jnp.int32)[None, :]
    live_mask = positions < lengths[page_request][:, None]
    page_max = jnp.max(jnp.where(live_mask[:, None, :], scores, far_below), axis=-1)
    weights = jnp.where(live_mask[:, None, :], jnp.exp(scores - page_max[..., None]), 0.0).astype(
        jnp.bfloat16
    )
    page_total = jnp.sum(weights.astype(jnp.float32), axis=-1)
    acc_blocks = jnp.einsum(
        "shp,spf->shf", weights, values_paged, preferred_element_type=jnp.float32
    )
    page_acc = jnp.sum(jnp.where(spread[None], acc_blocks, 0.0), axis=1)

    chosen = jnp.arange(requests, dtype=jnp.int32)[:, None] == owner_place[None, :]
    request_max = jnp.max(jnp.where(chosen[:, :, None], page_max[None, :, :], far_below), axis=1)
    factor = jnp.exp(page_max - request_max[owner_place])
    selector = chosen.astype(jnp.float32)
    request_total = jnp.dot(selector, page_total * factor, precision=lax.Precision.HIGHEST)
    request_acc = jnp.dot(
        selector, page_acc * spread_heads(factor, width_local), precision=lax.Precision.HIGHEST
    )
    packed = jnp.concatenate([request_acc, request_total, request_max], axis=1)
    packed = packed.reshape(lax.axis_size("seq"), rows, packed.shape[-1])
    home = scatter_xor(packed, "seq", width_local, heads_local)
    home_acc = home[:, :width_local]
    home_total = home[:, width_local : width_local + heads_local]
    home_max = home[:, width_local + heads_local :]
    final_max = jnp.maximum(home_max, own_score)
    stored_factor = jnp.exp(home_max - final_max)
    total_stored = home_total * stored_factor
    stored = home_acc * spread_heads(stored_factor, width_local)
    own_factor = jnp.exp(own_score - final_max)
    total = total_stored + own_factor
    summed = stored + value_own.astype(jnp.float32) * spread_heads(own_factor, width_local)
    attended = (summed / spread_heads(total, width_local)).astype(jnp.bfloat16)
    partial_out = jnp.dot(attended, output_weight, preferred_element_type=jnp.float32)
    attn_out = sum_radix(partial_out, "tensor")
    width = attn_out.shape[1]
    state = gathered.astype(jnp.float32)
    unit = attn_out / jnp.sqrt(jnp.sum(attn_out * attn_out, axis=-1, keepdims=True) / width + epsilon)
    mixed = state + eigen_rate * (unit - state)
    result = mixed / jnp.sqrt(jnp.sum(mixed * mixed, axis=-1, keepdims=True) / width + epsilon)
    first_col = lax.axis_index("tensor") * width_local
    return lax.dynamic_slice_in_dim(result, first_col, width_local, 1).astype(jnp.bfloat16)


def solution(mesh):
    placed = (
        P("seq", "tensor"),
        P(None, None, "tensor"),
        P("tensor", None),
        P("tensor"),
        P(),
        P(),
        P("seq"),
        P("seq"),
        P("seq", None, None, "tensor"),
    )
    return jax.shard_map(
        local, mesh=mesh, in_specs=placed, out_specs=P("seq", "tensor"), check_vma=False
    )
```
